256 devices in a mesh: scale: 16 (over x_hi, y, core), rt: 16 (over z, x_lo).
Axes of the slice: x: 4 (x_hi: 2, x_lo: 2; x = x_hi * 2 + x_lo), y: 4, z: 8, core: 2. Of those that a mesh axis runs over, the one named last changes fastest.
Arguments:
- slab: float32 [384, 128, 896], P('rt'), may hold values from -6 to 6
- widths: int32 [16], replicated, may hold values from 1 to 8
Outputs:
- peak: bfloat16 [384, 128, 896], P('rt', 'scale')
- energy: float32 [384, 128, 896], P('rt', 'scale')
The draws below stay inside these ranges and needn't reach their ends.
All inputs are finite; a program needn't handle non-finite values.
Results may differ from the reference program's by a relative error of at most 0.006.
Values may be sent and summed in bfloat16 or wider, within the bound.
No kernel may reach another device: no remote copies, remote signals or barrier semaphores. Data moves between devices by JAX's collectives and lax.ppermute only.
A program may use at most 128 MiB of HBM per device.

```python
import jax
import jax.numpy as jnp
from jax import lax

MZ = 128
SCANS = 896
SCAN_RATIO = 16
HALO = 24
WMAX = 8
FRAMES = 384
SCALES = 16


def plant(result, rng, smallest, high):
    dims = result.shape
    spot = [jax.random.randint(jax.random.fold_in(rng, axis), (), 0, dims[axis]) for axis in range(len(dims))]
    result = result.at[tuple(spot)].set(smallest)
    longest = dims.index(max(dims))
    spot[longest] = (spot[longest] + 1) % dims[longest]
    return result.at[tuple(spot)].set(high)


def steps_of(rng, dims, pieces, smallest, largest):
    level, own = 1.0, jax.random.fold_in(rng, 6)
    for position, blocks in pieces:
        steps = jnp.exp(jax.random.uniform(jax.random.fold_in(own, position), (blocks,), jnp.float32, smallest / len(pieces), largest / len(pieces)))
        level = level * jnp.repeat(steps, dims[position] // blocks).reshape([-1 if axis == position else 1 for axis in range(len(dims))])
    return level


def centred(rng, extent, scale, bound, shards=(), kind=jnp.bfloat16):
    result = jax.random.normal(rng, extent, jnp.float32) * scale
    if len(shards) > 0:
        result = steps_of(rng, extent, shards, -0.22, 0.18) * result
    return jnp.clip(result, min=-bound, max=bound).astype(kind)


def setup_inputs(seed: int = 0) -> dict:
    streams_of = jax.random.split(jax.random.key(seed), 3)
    slab = centred(streams_of[0], (FRAMES, MZ, SCANS), 1.0, 6.0, ((0, 16),), jnp.float32)
    widths = plant(jax.random.randint(streams_of[1], (SCALES,), 1, WMAX + 1), jax.random.fold_in(streams_of[1], 1), 1, WMAX).astype(jnp.int32)
    return dict(slab=slab, widths=widths)


def mexican(offsets, spread):
    ratio = offsets / spread
    return (1.0 - ratio * ratio) * jnp.exp(-0.5 * ratio * ratio) / jnp.sqrt(spread)

def to_bf16_and_back(values):
    return lax.optimization_barrier(values.astype(jnp.bfloat16)).astype(jnp.float32)

def reference(slab, widths):
    signal = to_bf16_and_back(slab)
    scan_pos = jnp.arange(SCANS, dtype=jnp.float32)
    scan_diff = scan_pos[:, None] - scan_pos[None, :]
    frame_pos = jnp.arange(FRAMES, dtype=jnp.float32)
    frame_diff = frame_pos[None, :] - frame_pos[:, None]
    inside = jnp.abs(frame_diff) <= HALO

    def one_scale(carry, width_value):
        best, total = carry
        scale_width = width_value.astype(jnp.float32)
        scan_table = to_bf16_and_back(mexican(scan_diff, SCAN_RATIO * scale_width))
        frame_table = to_bf16_and_back(jnp.where(inside, mexican(frame_diff, scale_width), 0.0))
        smooth = jnp.einsum('fms,st->fmt', signal, scan_table, precision=lax.Precision.HIGHEST)
        smooth = to_bf16_and_back(smooth)
        answer = jnp.einsum('fj,jmt->fmt', frame_table, smooth, precision=lax.Precision.HIGHEST)
        answer = to_bf16_and_back(answer)
        return ((jnp.maximum(best, answer), total + answer * answer), None)
    start = (jnp.full(slab.shape, -jnp.inf, jnp.float32), jnp.zeros(slab.shape, jnp.float32))
    (best, total), _ = lax.scan(one_scale, start, widths)
    return (best.astype(jnp.bfloat16), total)
```

```python
import jax
import jax.numpy as jnp
from jax import lax
from jax.sharding import PartitionSpec as P

SCAN_RATIO = 16
HALO = 24


def mexican(offsets, spread):
    ratio = offsets / spread
    return (1.0 - ratio * ratio) * jnp.exp(-0.5 * ratio * ratio) / jnp.sqrt(spread)


def neighbours(block, axis):
    count = lax.axis_size(axis)
    forward = [(i, i + 1) for i in range(count - 1)]
    backward = [(i + 1, i) for i in range(count - 1)]
    frames = block.shape[0]
    low = lax.ppermute(lax.slice_in_dim(block, frames - HALO, frames, axis=0), axis, forward)
    high = lax.ppermute(lax.slice_in_dim(block, 0, HALO, axis=0), axis, backward)
    return low, high


def frame_tables(frames, scale_widths):
    out_pos = jnp.arange(frames, dtype=jnp.float32)
    in_pos = jnp.arange(frames + 2 * HALO, dtype=jnp.float32) - HALO
    offsets = (in_pos[None, :] - out_pos[:, None])[None]
    spread = scale_widths[:, None, None]
    values = jnp.where(jnp.abs(offsets) <= HALO, mexican(offsets, spread), 0.0)
    return values.astype(jnp.bfloat16)


def scan_tables(scans, scale_widths):
    positions = jnp.arange(scans, dtype=jnp.float32)
    offsets = (positions[:, None] - positions[None, :])[None]
    spread = SCAN_RATIO * scale_widths[:, None, None]
    return mexican(offsets, spread).astype(jnp.bfloat16)


def per_device(slab, widths):
    frames, mz_bins, scans = slab.shape
    strip = mz_bins // lax.axis_size("scale")
    first = lax.axis_index("scale") * strip
    signal = lax.dynamic_slice_in_dim(slab, first, strip, axis=1).astype(jnp.bfloat16)
    low, high = neighbours(signal, "rt")
    padded = jnp.concatenate([low, signal, high], axis=0).reshape(frames + 2 * HALO, strip * scans)
    scale_widths = widths.astype(jnp.float32)
    count = scale_widths.shape[0]
    framed = jnp.einsum(
        "cfj,jn->cfn", frame_tables(frames, scale_widths), padded, preferred_element_type=jnp.float32
    ).astype(jnp.bfloat16)
    framed = framed.reshape(count, frames * strip, scans)
    answer = jnp.einsum(
        "cms,cst->cmt", framed, scan_tables(scans, scale_widths), preferred_element_type=jnp.float32
    ).astype(jnp.bfloat16)
    peak = jnp.max(answer, axis=0).reshape(frames, strip, scans)
    energy = jnp.sum(jnp.square(answer.astype(jnp.float32)), axis=0).reshape(frames, strip, scans)
    return (peak, energy)


def solution(mesh):
    in_specs = (P("rt", None, None), P())
    out_specs = (P("rt", "scale", None), P("rt", "scale", None))
    return jax.shard_map(
        per_device, mesh=mesh, in_specs=in_specs, out_specs=out_specs, check_vma=False
    )
```

```python
import jax
import jax.numpy as jnp
from jax import lax
from jax.experimental import pallas as pl
from jax.experimental.pallas import tpu as pltpu
from jax.sharding import PartitionSpec as P

SCAN_RATIO = 16
HALO = 24
TILE = 128


def mexican(offsets, spread):
    ratio = offsets / spread
    return (1.0 - ratio * ratio) * jnp.exp(-0.5 * ratio * ratio) / jnp.sqrt(spread)


def neighbours(block, axis):
    count = lax.axis_size(axis)
    forward = [(i, i + 1) for i in range(count - 1)]
    backward = [(i + 1, i) for i in range(count - 1)]
    frames = block.shape[0]
    low = lax.ppermute(lax.slice_in_dim(block, frames - HALO, frames, axis=0), axis, forward)
    high = lax.ppermute(lax.slice_in_dim(block, 0, HALO, axis=0), axis, backward)
    return low, high


def frame_tables(frames, scale_widths, depth):
    out_pos = jnp.arange(frames, dtype=jnp.float32)
    in_pos = jnp.arange(depth, dtype=jnp.float32) - HALO
    offsets = (in_pos[None, :] - out_pos[:, None])[None]
    spread = scale_widths[:, None, None]
    inside = (jnp.abs(offsets) <= HALO) & (in_pos < frames + HALO)[None, None, :]
    values = jnp.where(inside, mexican(offsets, spread), 0.0)
    return values.astype(jnp.bfloat16).reshape(-1, depth)


def scan_blocks(scans, scale_widths):
    nb = scans // TILE
    shift = (jnp.arange(2 * nb - 1, dtype=jnp.float32) - (nb - 1)) * TILE
    pos = jnp.arange(TILE, dtype=jnp.float32)
    offsets = shift[:, None, None] + (pos[:, None] - pos[None, :])[None]
    spread = SCAN_RATIO * scale_widths[:, None, None, None]
    return mexican(offsets[None], spread).astype(jnp.bfloat16)


def wavelet_kernel(f_ref, p_ref, b_ref, peak_ref, energy_ref, g_scr, s_scr):
    c = pl.program_id(0)
    count, rows, scans = g_scr.shape
    frames = f_ref.shape[0] // count
    strip = rows // frames
    nb = scans // TILE

    @pl.when(c == 0)
    def _():
        fall = f_ref[...]
        for m in range(strip):
            gm = jnp.dot(fall, p_ref[:, m * scans:(m + 1) * scans], preferred_element_type=jnp.float32)
            for cc in range(count):
                g_scr[cc, m * frames:(m + 1) * frames, :] = gm[cc * frames:(cc + 1) * frames, :]

    for i in range(nb):
        for j in range(nb):
            s_scr[i * TILE:(i + 1) * TILE, j * TILE:(j + 1) * TILE] = b_ref[0, i - j + nb - 1]
    lhs = g_scr[c].astype(jnp.bfloat16)
    answer = jnp.dot(lhs, s_scr[...], preferred_element_type=jnp.float32).astype(jnp.bfloat16)
    square = jnp.square(answer.astype(jnp.float32))

    @pl.when(c == 0)
    def _():
        peak_ref[...] = answer
        energy_ref[...] = square

    @pl.when(c > 0)
    def _():
        peak_ref[...] = jnp.maximum(peak_ref[...], answer)
        energy_ref[...] = energy_ref[...] + square


def wavelet_core(ftab, padded, blocks, frames, strip, scans, interpret=False):
    count = blocks.shape[0]
    depth = padded.shape[0]
    rows = frames * strip
    nblk = blocks.shape[1]
    return pl.pallas_call(
        wavelet_kernel,
        grid=(count,),
        in_specs=[
            pl.BlockSpec((count * frames, depth), lambda c: (0, 0)),
            pl.BlockSpec((depth, strip * scans), lambda c: (0, 0)),
            pl.BlockSpec((1, nblk, TILE, TILE), lambda c: (c, 0, 0, 0)),
        ],
        out_specs=[
            pl.BlockSpec((rows, scans), lambda c: (0, 0)),
            pl.BlockSpec((rows, scans), lambda c: (0, 0)),
        ],
        out_shape=[
            jax.ShapeDtypeStruct((rows, scans), jnp.bfloat16),
            jax.ShapeDtypeStruct((rows, scans), jnp.float32),
        ],
        scratch_shapes=[
            pltpu.VMEM((count, rows, scans), jnp.float32),
            pltpu.VMEM((scans, scans), jnp.bfloat16),
        ],
        compiler_params=pltpu.CompilerParams(
            dimension_semantics=("arbitrary",), vmem_limit_bytes=56 * 1024 * 1024
        ),
        interpret=interpret,
    )(ftab, padded, blocks)


def compute(signal, low, high, widths, interpret=False):
    frames, strip, scans = signal.shape
    depth = -(-(frames + 2 * HALO) // TILE) * TILE
    pad = jnp.zeros((depth - frames - 2 * HALO, strip, scans), signal.dtype)
    padded = jnp.concatenate([low, signal, high, pad], axis=0).reshape(depth, strip * scans)
    scale_widths = widths.astype(jnp.float32)
    ftab = frame_tables(frames, scale_widths, depth)
    blocks = scan_blocks(scans, scale_widths)
    peak, energy = wavelet_core(ftab, padded, blocks, frames, strip, scans, interpret)
    peak = peak.reshape(strip, frames, scans).transpose(1, 0, 2)
    energy = energy.reshape(strip, frames, scans).transpose(1, 0, 2)
    return peak, energy


def per_device(slab, widths):
    frames, mz_bins, scans = slab.shape
    strip = mz_bins // lax.axis_size("scale")
    first = lax.axis_index("scale") * strip
    signal = lax.dynamic_slice_in_dim(slab, first, strip, axis=1).astype(jnp.bfloat16)
    low, high = neighbours(signal, "rt")
    return compute(signal, low, high, widths)


def solution(mesh):
    in_specs = (P("rt", None, None), P())
    out_specs = (P("rt", "scale", None), P("rt", "scale", None))
    return jax.shard_map(
        per_device, mesh=mesh, in_specs=in_specs, out_specs=out_specs, check_vma=False
    )
```

```python
import jax
import jax.numpy as jnp
from jax import lax
from jax.experimental import pallas as pl
from jax.experimental.pallas import tpu as pltpu
from jax.sharding import PartitionSpec as P

SCAN_RATIO = 16
HALO = 24
TILE = 128


def mexican(offsets, spread):
    ratio = offsets / spread
    return (1.0 - ratio * ratio) * jnp.exp(-0.5 * ratio * ratio) / jnp.sqrt(spread)


def halos(slab, strip):
    n_scale, n_rt = lax.axis_size("scale"), lax.axis_size("rt")
    half = n_scale // 2
    s, r = lax.axis_index("scale"), lax.axis_index("rt")
    other = (s + half) % n_scale
    forward, backward = [], []
    for ss in range(n_scale):
        for rr in range(n_rt):
            flip = (ss + half) % n_scale
            if rr + 1 < n_rt:
                forward.append((ss * n_rt + rr, (ss if rr % 2 == 0 else flip) * n_rt + rr + 1))
            if rr > 0:
                backward.append((ss * n_rt + rr, (ss if rr % 2 == 1 else flip) * n_rt + rr - 1))
    frames = slab.shape[0]

    def piece(index, start):
        part = lax.dynamic_slice_in_dim(slab, index * strip, strip, axis=1)
        part = lax.slice_in_dim(part, start, start + HALO, axis=0)
        return part.astype(jnp.bfloat16)

    send_fwd = piece(jnp.where(r % 2 == 0, s, other), frames - HALO)
    send_bwd = piece(jnp.where(r % 2 == 1, s, other), 0)
    low = lax.ppermute(send_fwd, ("scale", "rt"), forward)
    high = lax.ppermute(send_bwd, ("scale", "rt"), backward)
    return low, high


def frame_tables(frames, scale_widths, depth):
    out_pos = jnp.arange(frames, dtype=jnp.float32)
    in_pos = jnp.arange(depth, dtype=jnp.float32) - HALO
    offsets = (in_pos[None, :] - out_pos[:, None])[None]
    spread = scale_widths[:, None, None]
    inside = (jnp.abs(offsets) <= HALO) & (in_pos < frames + HALO)[None, None, :]
    values = jnp.where(inside, mexican(offsets, spread), 0.0)
    return values.astype(jnp.bfloat16).reshape(-1, depth)


def scan_blocks(scans, scale_widths):
    nb = scans // TILE
    shift = (jnp.arange(2 * nb - 1, dtype=jnp.float32) - (nb - 1)) * TILE
    pos = jnp.arange(TILE, dtype=jnp.float32)
    offsets = shift[:, None, None] + (pos[:, None] - pos[None, :])[None]
    spread = SCAN_RATIO * scale_widths[:, None, None, None]
    return mexican(offsets[None], spread).astype(jnp.bfloat16)


def wavelet_kernel(f_ref, lo_ref, own_ref, hi_ref, b_ref, peak_ref, energy_ref, p_scr, g_scr, s_scr):
    c = pl.program_id(0)
    count, frames, strip, scans = g_scr.shape
    rows = frames * strip
    nb = scans // TILE

    @pl.when(c == 0)
    def _():
        p_scr[...] = jnp.zeros(p_scr.shape, p_scr.dtype)
        for m in range(strip):
            cols = slice(m * scans, (m + 1) * scans)
            p_scr[0:HALO, cols] = lo_ref[:, m, :].astype(jnp.float32)
            p_scr[HALO:HALO + frames, cols] = own_ref[:, m, :].astype(jnp.float32)
            p_scr[HALO + frames:2 * HALO + frames, cols] = hi_ref[:, m, :].astype(jnp.float32)
        fall = f_ref[...]
        for m in range(strip):
            part = p_scr[:, m * scans:(m + 1) * scans].astype(jnp.bfloat16)
            gm = jnp.dot(fall, part, preferred_element_type=jnp.float32)
            for cc in range(count):
                g_scr[cc, :, m, :] = gm[cc * frames:(cc + 1) * frames, :]

    for i in range(nb):
        for j in range(nb):
            s_scr[i * TILE:(i + 1) * TILE, j * TILE:(j + 1) * TILE] = b_ref[0, i - j + nb - 1]
    lhs = g_scr[c].reshape(rows, scans).astype(jnp.bfloat16)
    answer = jnp.dot(lhs, s_scr[...], preferred_element_type=jnp.float32).astype(jnp.bfloat16)
    square = jnp.square(answer.astype(jnp.float32))

    @pl.when(c == 0)
    def _():
        peak_ref[...] = answer
        energy_ref[...] = square

    @pl.when(c > 0)
    def _():
        peak_ref[...] = jnp.maximum(peak_ref[...], answer)
        energy_ref[...] = energy_ref[...] + square


def wavelet_core(ftab, low, own, high, blocks, frames, strip, scans, interpret=False):
    count = blocks.shape[0]
    depth = ftab.shape[1]
    rows = frames * strip
    nblk = blocks.shape[1]
    whole = lambda c: (0, 0)
    whole3 = lambda c: (0, 0, 0)
    return pl.pallas_call(
        wavelet_kernel,
        grid=(count,),
        in_specs=[
            pl.BlockSpec((count * frames, depth), whole),
            pl.BlockSpec((HALO, strip, scans), whole3),
            pl.BlockSpec((frames, strip, scans), whole3),
            pl.BlockSpec((HALO, strip, scans), whole3),
            pl.BlockSpec((1, nblk, TILE, TILE), lambda c: (c, 0, 0, 0)),
        ],
        out_specs=[
            pl.BlockSpec((rows, scans), whole),
            pl.BlockSpec((rows, scans), whole),
        ],
        out_shape=[
            jax.ShapeDtypeStruct((rows, scans), jnp.bfloat16),
            jax.ShapeDtypeStruct((rows, scans), jnp.float32),
        ],
        scratch_shapes=[
            pltpu.VMEM((depth, strip * scans), jnp.float32),
            pltpu.VMEM((count, frames, strip, scans), jnp.float32),
            pltpu.VMEM((scans, scans), jnp.bfloat16),
        ],
        compiler_params=pltpu.CompilerParams(
            dimension_semantics=("arbitrary",), vmem_limit_bytes=56 * 1024 * 1024
        ),
        interpret=interpret,
    )(ftab, low, own, high, blocks)


def compute(own, low, high, widths, interpret=False):
    frames, strip, scans = own.shape
    depth = -(-(frames + 2 * HALO) // TILE) * TILE
    scale_widths = widths.astype(jnp.float32)
    ftab = frame_tables(frames, scale_widths, depth)
    blocks = scan_blocks(scans, scale_widths)
    peak, energy = wavelet_core(ftab, low, own, high, blocks, frames, strip, scans, interpret)
    return peak.reshape(frames, strip, scans), energy.reshape(frames, strip, scans)


def per_device(slab, widths):
    frames, mz_bins, scans = slab.shape
    strip = mz_bins // lax.axis_size("scale")
    first = lax.axis_index("scale") * strip
    own = lax.dynamic_slice_in_dim(slab, first, strip, axis=1).astype(jnp.bfloat16)
    low, high = halos(slab, strip)
    return compute(own, low, high, widths)


def solution(mesh):
    in_specs = (P("rt", None, None), P())
    out_specs = (P("rt", "scale", None), P("rt", "scale", None))
    return jax.shard_map(
        per_device, mesh=mesh, in_specs=in_specs, out_specs=out_specs, check_vma=False
    )
```

```python
import jax
import jax.numpy as jnp
from jax import lax
from jax.experimental import pallas as pl
from jax.experimental.pallas import tpu as pltpu
from jax.sharding import PartitionSpec as P

SCAN_RATIO = 16
HALO = 24
TILE = 128


def mexican(offsets, spread):
    ratio = offsets / spread
    return (1.0 - ratio * ratio) * jnp.exp(-0.5 * ratio * ratio) / jnp.sqrt(spread)


def halos(slab, strip):
    n_scale, n_rt = lax.axis_size("scale"), lax.axis_size("rt")
    half = n_scale // 2
    s, r = lax.axis_index("scale"), lax.axis_index("rt")
    other = (s + half) % n_scale
    forward, backward = [], []
    for ss in range(n_scale):
        for rr in range(n_rt):
            flip = (ss + half) % n_scale
            if rr + 1 < n_rt:
                forward.append((ss * n_rt + rr, (ss if rr % 2 == 0 else flip) * n_rt + rr + 1))
            if rr > 0:
                backward.append((ss * n_rt + rr, (ss if rr % 2 == 1 else flip) * n_rt + rr - 1))
    frames = slab.shape[0]

    def piece(index, start):
        part = lax.dynamic_slice_in_dim(slab, index * strip, strip, axis=1)
        part = lax.slice_in_dim(part, start, start + HALO, axis=0)
        return part.astype(jnp.bfloat16)

    send_fwd = piece(jnp.where(r % 2 == 0, s, other), frames - HALO)
    send_bwd = piece(jnp.where(r % 2 == 1, s, other), 0)
    low = lax.ppermute(send_fwd, ("scale", "rt"), forward)
    high = lax.ppermute(send_bwd, ("scale", "rt"), backward)
    return low, high


def frame_tables(frames, scale_widths, depth):
    out_pos = jnp.arange(frames, dtype=jnp.float32)
    in_pos = jnp.arange(depth, dtype=jnp.float32) - HALO
    offsets = (in_pos[None, :] - out_pos[:, None])[None]
    spread = scale_widths[:, None, None]
    inside = (jnp.abs(offsets) <= HALO) & (in_pos < frames + HALO)[None, None, :]
    values = jnp.where(inside, mexican(offsets, spread), 0.0)
    return values.astype(jnp.bfloat16).reshape(-1, depth)


def scan_blocks(scans, scale_widths):
    nb = scans // TILE
    shift = (jnp.arange(2 * nb - 1, dtype=jnp.float32) - (nb - 1)) * TILE
    pos = jnp.arange(TILE, dtype=jnp.float32)
    offsets = shift[:, None, None] + (pos[:, None] - pos[None, :])[None]
    spread = SCAN_RATIO * scale_widths[:, None, None, None]
    return mexican(offsets[None], spread).astype(jnp.bfloat16)


def wavelet_kernel(f_ref, lo_ref, own_ref, hi_ref, b_ref, peak_ref, energy_ref,
                   p_scr, g_scr, s_scr, best_scr, total_scr):
    c = pl.program_id(0)
    count, rows, scans = g_scr.shape
    frames, strip, _ = own_ref.shape
    nb = scans // TILE
    used = 2 * HALO + frames

    @pl.when(c == 0)
    def _():
        p_scr[used:, :] = jnp.zeros((p_scr.shape[0] - used, p_scr.shape[1]), p_scr.dtype)
        for m in range(strip):
            cols = slice(m * scans, (m + 1) * scans)
            p_scr[0:HALO, cols] = lo_ref[:, m, :].astype(jnp.float32)
            p_scr[HALO:HALO + frames, cols] = own_ref[:, m, :].astype(jnp.float32)
            p_scr[HALO + frames:used, cols] = hi_ref[:, m, :].astype(jnp.float32)
        fall = f_ref[...]
        for m in range(strip):
            part = p_scr[:, m * scans:(m + 1) * scans].astype(jnp.bfloat16)
            gm = jnp.dot(fall, part, preferred_element_type=jnp.float32)
            for cc in range(count):
                g_scr[cc, m * frames:(m + 1) * frames, :] = gm[cc * frames:(cc + 1) * frames, :]

    for i in range(nb):
        for j in range(nb):
            s_scr[i * TILE:(i + 1) * TILE, j * TILE:(j + 1) * TILE] = b_ref[0, i - j + nb - 1]
    lhs = g_scr[c].astype(jnp.bfloat16)
    answer = jnp.dot(lhs, s_scr[...], preferred_element_type=jnp.float32).astype(jnp.bfloat16)
    answer = answer.astype(jnp.float32)
    square = answer * answer

    @pl.when(c == 0)
    def _():
        best_scr[...] = answer
        total_scr[...] = square

    @pl.when(c > 0)
    def _():
        best_scr[...] = jnp.maximum(best_scr[...], answer)
        total_scr[...] = total_scr[...] + square

    @pl.when(c == count - 1)
    def _():
        for m in range(strip):
            peak_ref[:, m, :] = best_scr[m * frames:(m + 1) * frames, :].astype(peak_ref.dtype)
            energy_ref[:, m, :] = total_scr[m * frames:(m + 1) * frames, :]


def wavelet_core(ftab, low, own, high, blocks, frames, strip, scans, interpret=False):
    count = blocks.shape[0]
    depth = ftab.shape[1]
    rows = frames * strip
    nblk = blocks.shape[1]
    whole = lambda c: (0, 0)
    whole3 = lambda c: (0, 0, 0)
    return pl.pallas_call(
        wavelet_kernel,
        grid=(count,),
        in_specs=[
            pl.BlockSpec((count * frames, depth), whole),
            pl.BlockSpec((HALO, strip, scans), whole3),
            pl.BlockSpec((frames, strip, scans), whole3),
            pl.BlockSpec((HALO, strip, scans), whole3),
            pl.BlockSpec((1, nblk, TILE, TILE), lambda c: (c, 0, 0, 0)),
        ],
        out_specs=[
            pl.BlockSpec((frames, strip, scans), whole3),
            pl.BlockSpec((frames, strip, scans), whole3),
        ],
        out_shape=[
            jax.ShapeDtypeStruct((frames, strip, scans), jnp.bfloat16),
            jax.ShapeDtypeStruct((frames, strip, scans), jnp.float32),
        ],
        scratch_shapes=[
            pltpu.VMEM((depth, strip * scans), jnp.float32),
            pltpu.VMEM((count, rows, scans), jnp.float32),
            pltpu.VMEM((scans, scans), jnp.bfloat16),
            pltpu.VMEM((rows, scans), jnp.float32),
            pltpu.VMEM((rows, scans), jnp.float32),
        ],
        compiler_params=pltpu.CompilerParams(
            dimension_semantics=("arbitrary",), vmem_limit_bytes=56 * 1024 * 1024
        ),
        interpret=interpret,
    )(ftab, low, own, high, blocks)


def compute(own, low, high, widths, interpret=False):
    frames, strip, scans = own.shape
    depth = -(-(frames + 2 * HALO) // TILE) * TILE
    scale_widths = widths.astype(jnp.float32)
    ftab = frame_tables(frames, scale_widths, depth)
    blocks = scan_blocks(scans, scale_widths)
    return wavelet_core(ftab, low, own, high, blocks, frames, strip, scans, interpret)


def per_device(slab, widths):
    frames, mz_bins, scans = slab.shape
    strip = mz_bins // lax.axis_size("scale")
    first = lax.axis_index("scale") * strip
    own = lax.dynamic_slice_in_dim(slab, first, strip, axis=1).astype(jnp.bfloat16)
    low, high = halos(slab, strip)
    return compute(own, low, high, widths)


def solution(mesh):
    in_specs = (P("rt", None, None), P())
    out_specs = (P("rt", "scale", None), P("rt", "scale", None))
    return jax.shard_map(
        per_device, mesh=mesh, in_specs=in_specs, out_specs=out_specs, check_vma=False
    )
```

```python
import jax
import jax.numpy as jnp
from jax import lax
from jax.experimental import pallas as pl
from jax.experimental.pallas import tpu as pltpu
from jax.sharding import PartitionSpec as P

SCAN_RATIO = 16
HALO = 24
TILE = 128


def mexican(offsets, spread):
    ratio = offsets / spread
    return (1.0 - ratio * ratio) * jnp.exp(-0.5 * ratio * ratio) / jnp.sqrt(spread)


def halos(slab, strip):
    n_scale, n_rt = lax.axis_size("scale"), lax.axis_size("rt")
    half = n_scale // 2
    s, r = lax.axis_index("scale"), lax.axis_index("rt")
    other = (s + half) % n_scale
    forward, backward = [], []
    for ss in range(n_scale):
        for rr in range(n_rt):
            flip = (ss + half) % n_scale
            if rr + 1 < n_rt:
                forward.append((ss * n_rt + rr, (ss if rr % 2 == 0 else flip) * n_rt + rr + 1))
            if rr > 0:
                backward.append((ss * n_rt + rr, (ss if rr % 2 == 1 else flip) * n_rt + rr - 1))
    frames = slab.shape[0]

    def piece(index, start):
        part = lax.dynamic_slice_in_dim(slab, index * strip, strip, axis=1)
        part = lax.slice_in_dim(part, start, start + HALO, axis=0)
        return part.astype(jnp.bfloat16)

    send_fwd = piece(jnp.where(r % 2 == 0, s, other), frames - HALO)
    send_bwd = piece(jnp.where(r % 2 == 1, s, other), 0)
    low = lax.ppermute(send_fwd, ("scale", "rt"), forward)
    high = lax.ppermute(send_bwd, ("scale", "rt"), backward)
    return low, high


def frame_tables(frames, scale_widths, depth):
    out_pos = jnp.arange(frames, dtype=jnp.float32)
    in_pos = jnp.arange(depth, dtype=jnp.float32) - HALO
    offsets = (in_pos[None, :] - out_pos[:, None])[None]
    spread = scale_widths[:, None, None]
    inside = (jnp.abs(offsets) <= HALO) & (in_pos < frames + HALO)[None, None, :]
    values = jnp.where(inside, mexican(offsets, spread), 0.0)
    return values.astype(jnp.bfloat16).reshape(-1, depth)


def scan_blocks(scans, scale_widths):
    nb = scans // TILE
    shift = (jnp.arange(2 * nb - 1, dtype=jnp.float32) - (nb - 1)) * TILE
    pos = jnp.arange(TILE, dtype=jnp.float32)
    offsets = shift[:, None, None] + (pos[:, None] - pos[None, :])[None]
    spread = SCAN_RATIO * scale_widths[:, None, None, None]
    return mexican(offsets[None], spread).astype(jnp.bfloat16)


def wavelet_kernel(strip_ref, f_ref, lo_ref, own_ref, hi_ref, b_ref, peak_ref, energy_ref,
                   p_scr, g_scr, s_scr, best_scr, total_scr):
    c = pl.program_id(0)
    count, rows, scans = g_scr.shape
    frames, strip, _ = own_ref.shape
    nb = scans // TILE
    used = 2 * HALO + frames

    @pl.when(c == 0)
    def _():
        p_scr[used:, :] = jnp.zeros((p_scr.shape[0] - used, p_scr.shape[1]), p_scr.dtype)
        for m in range(strip):
            cols = slice(m * scans, (m + 1) * scans)
            p_scr[0:HALO, cols] = lo_ref[:, m, :].astype(jnp.float32)
            p_scr[HALO:HALO + frames, cols] = own_ref[:, m, :]
            p_scr[HALO + frames:used, cols] = hi_ref[:, m, :].astype(jnp.float32)
        fall = f_ref[...]
        for m in range(strip):
            part = p_scr[:, m * scans:(m + 1) * scans].astype(jnp.bfloat16)
            gm = jnp.dot(fall, part, preferred_element_type=jnp.float32)
            for cc in range(count):
                g_scr[cc, m * frames:(m + 1) * frames, :] = gm[cc * frames:(cc + 1) * frames, :]

    for i in range(nb):
        for j in range(nb):
            s_scr[i * TILE:(i + 1) * TILE, j * TILE:(j + 1) * TILE] = b_ref[0, i - j + nb - 1]
    lhs = g_scr[c].astype(jnp.bfloat16)
    answer = jnp.dot(lhs, s_scr[...], preferred_element_type=jnp.float32).astype(jnp.bfloat16)
    answer = answer.astype(jnp.float32)
    square = answer * answer

    @pl.when(c == 0)
    def _():
        best_scr[...] = answer
        total_scr[...] = square

    @pl.when(c > 0)
    def _():
        best_scr[...] = jnp.maximum(best_scr[...], answer)
        total_scr[...] = total_scr[...] + square

    @pl.when(c == count - 1)
    def _():
        for m in range(strip):
            peak_ref[:, m, :] = best_scr[m * frames:(m + 1) * frames, :].astype(peak_ref.dtype)
            energy_ref[:, m, :] = total_scr[m * frames:(m + 1) * frames, :]


def wavelet_core(first, ftab, low, slab, high, blocks, interpret=False):
    count = blocks.shape[0]
    depth = ftab.shape[1]
    frames, strip, scans = low.shape
    rows = frames * strip
    nblk = blocks.shape[1]
    whole = lambda c, i: (0, 0)
    whole3 = lambda c, i: (0, 0, 0)
    grid_spec = pltpu.PrefetchScalarGridSpec(
        num_scalar_prefetch=1,
        grid=(count,),
        in_specs=[
            pl.BlockSpec((count * frames, depth), whole),
            pl.BlockSpec((HALO, strip, scans), whole3),
            pl.BlockSpec((frames, strip, scans), lambda c, i: (0, i[0], 0)),
            pl.BlockSpec((HALO, strip, scans), whole3),
            pl.BlockSpec((1, nblk, TILE, TILE), lambda c, i: (c, 0, 0, 0)),
        ],
        out_specs=[
            pl.BlockSpec((frames, strip, scans), whole3),
            pl.BlockSpec((frames, strip, scans), whole3),
        ],
        scratch_shapes=[
            pltpu.VMEM((depth, strip * scans), jnp.float32),
            pltpu.VMEM((count, rows, scans), jnp.float32),
            pltpu.VMEM((scans, scans), jnp.bfloat16),
            pltpu.VMEM((rows, scans), jnp.float32),
            pltpu.VMEM((rows, scans), jnp.float32),
        ],
    )
    return pl.pallas_call(
        wavelet_kernel,
        grid_spec=grid_spec,
        out_shape=[
            jax.ShapeDtypeStruct((frames, strip, scans), jnp.bfloat16),
            jax.ShapeDtypeStruct((frames, strip, scans), jnp.float32),
        ],
        compiler_params=pltpu.CompilerParams(
            dimension_semantics=("arbitrary",), vmem_limit_bytes=56 * 1024 * 1024
        ),
        interpret=interpret,
    )(first, ftab, low, slab, high, blocks)


def compute(slab, block_index, low, high, widths, interpret=False):
    frames, strip, scans = low.shape
    depth = -(-(frames + 2 * HALO) // TILE) * TILE
    scale_widths = widths.astype(jnp.float32)
    ftab = frame_tables(frames, scale_widths, depth)
    blocks = scan_blocks(scans, scale_widths)
    first = jnp.reshape(block_index, (1,)).astype(jnp.int32)
    return wavelet_core(first, ftab, low, slab, high, blocks, interpret)


def per_device(slab, widths):
    strip = slab.shape[1] // lax.axis_size("scale")
    low, high = halos(slab, strip)
    return compute(slab, lax.axis_index("scale"), low, high, widths)


def solution(mesh):
    in_specs = (P("rt", None, None), P())
    out_specs = (P("rt", "scale", None), P("rt", "scale", None))
    return jax.shard_map(
        per_device, mesh=mesh, in_specs=in_specs, out_specs=out_specs, check_vma=False
    )
```

```python
import jax
import jax.numpy as jnp
from jax import lax
from jax.experimental import pallas as pl
from jax.experimental.pallas import tpu as pltpu
from jax.sharding import PartitionSpec as P

SCAN_RATIO = 16
HALO = 24
TILE = 128


def mexican(offsets, spread):
    ratio = offsets / spread
    return (1.0 - ratio * ratio) * jnp.exp(-0.5 * ratio * ratio) / jnp.sqrt(spread)


def halos(slab, strip):
    n_scale, n_rt = lax.axis_size("scale"), lax.axis_size("rt")
    half = n_scale // 2
    s, r = lax.axis_index("scale"), lax.axis_index("rt")
    other = (s + half) % n_scale
    forward, backward = [], []
    for ss in range(n_scale):
        for rr in range(n_rt):
            flip = (ss + half) % n_scale
            if rr + 1 < n_rt:
                forward.append((ss * n_rt + rr, (ss if rr % 2 == 0 else flip) * n_rt + rr + 1))
            if rr > 0:
                backward.append((ss * n_rt + rr, (ss if rr % 2 == 1 else flip) * n_rt + rr - 1))
    frames = slab.shape[0]

    def piece(index, start):
        part = lax.dynamic_slice_in_dim(slab, index * strip, strip, axis=1)
        part = lax.slice_in_dim(part, start, start + HALO, axis=0)
        return part.astype(jnp.bfloat16)

    send_fwd = piece(jnp.where(r % 2 == 0, s, other), frames - HALO)
    send_bwd = piece(jnp.where(r % 2 == 1, s, other), 0)
    low = lax.ppermute(send_fwd, ("scale", "rt"), forward)
    high = lax.ppermute(send_bwd, ("scale", "rt"), backward)
    return low, high


def frame_tables(frames, scale_widths, depth):
    out_pos = jnp.arange(frames, dtype=jnp.float32)
    in_pos = jnp.arange(depth, dtype=jnp.float32) - HALO
    offsets = (in_pos[None, :] - out_pos[:, None])[None]
    spread = scale_widths[:, None, None]
    inside = (jnp.abs(offsets) <= HALO) & (in_pos < frames + HALO)[None, None, :]
    values = jnp.where(inside, mexican(offsets, spread), 0.0)
    return values.astype(jnp.bfloat16).reshape(-1, depth)


def scan_blocks(scans, scale_widths):
    nb = scans // TILE
    shift = (jnp.arange(2 * nb - 1, dtype=jnp.float32) - (nb - 1)) * TILE
    pos = jnp.arange(TILE, dtype=jnp.float32)
    offsets = shift[:, None, None] + (pos[:, None] - pos[None, :])[None]
    spread = SCAN_RATIO * scale_widths[:, None, None, None]
    return mexican(offsets[None], spread).astype(jnp.bfloat16)


def wavelet_kernel(strip_ref, f_ref, lo_ref, own_ref, hi_ref, b_ref, peak_ref, energy_ref,
                   p_scr, g_scr, s_scr, best_scr, total_scr):
    count, rows, scans = g_scr.shape
    frames, strip, _ = own_ref.shape
    nb = scans // TILE
    used = 2 * HALO + frames

    p_scr[used:, :] = jnp.zeros((p_scr.shape[0] - used, p_scr.shape[1]), p_scr.dtype)
    for m in range(strip):
        cols = slice(m * scans, (m + 1) * scans)
        p_scr[0:HALO, cols] = lo_ref[:, m, :].astype(jnp.float32)
        p_scr[HALO:HALO + frames, cols] = own_ref[:, m, :]
        p_scr[HALO + frames:used, cols] = hi_ref[:, m, :].astype(jnp.float32)
    fall = f_ref[...]
    for m in range(strip):
        part = p_scr[:, m * scans:(m + 1) * scans].astype(jnp.bfloat16)
        gm = jnp.dot(fall, part, preferred_element_type=jnp.float32)
        for cc in range(count):
            g_scr[cc, m * frames:(m + 1) * frames, :] = gm[cc * frames:(cc + 1) * frames, :]

    for c in range(count):
        table = s_scr.at[c % 2]
        for i in range(nb):
            for j in range(nb):
                table[i * TILE:(i + 1) * TILE, j * TILE:(j + 1) * TILE] = b_ref[c, i - j + nb - 1]
        lhs = g_scr[c].astype(jnp.bfloat16)
        answer = jnp.dot(lhs, table[...], preferred_element_type=jnp.float32).astype(jnp.bfloat16)
        answer = answer.astype(jnp.float32)
        if c == 0:
            best_scr[...] = answer
            total_scr[...] = answer * answer
        else:
            best_scr[...] = jnp.maximum(best_scr[...], answer)
            total_scr[...] = total_scr[...] + answer * answer

    for m in range(strip):
        peak_ref[:, m, :] = best_scr[m * frames:(m + 1) * frames, :].astype(peak_ref.dtype)
        energy_ref[:, m, :] = total_scr[m * frames:(m + 1) * frames, :]


def wavelet_core(first, ftab, low, slab, high, blocks, interpret=False):
    count = blocks.shape[0]
    depth = ftab.shape[1]
    frames, strip, scans = low.shape
    rows = frames * strip
    nblk = blocks.shape[1]
    whole = lambda c, i: (0, 0)
    whole3 = lambda c, i: (0, 0, 0)
    grid_spec = pltpu.PrefetchScalarGridSpec(
        num_scalar_prefetch=1,
        grid=(1,),
        in_specs=[
            pl.BlockSpec((count * frames, depth), whole),
            pl.BlockSpec((HALO, strip, scans), whole3),
            pl.BlockSpec((frames, strip, scans), lambda c, i: (0, i[0], 0)),
            pl.BlockSpec((HALO, strip, scans), whole3),
            pl.BlockSpec((count, nblk, TILE, TILE), lambda c, i: (0, 0, 0, 0)),
        ],
        out_specs=[
            pl.BlockSpec((frames, strip, scans), whole3),
            pl.BlockSpec((frames, strip, scans), whole3),
        ],
        scratch_shapes=[
            pltpu.VMEM((depth, strip * scans), jnp.float32),
            pltpu.VMEM((count, rows, scans), jnp.float32),
            pltpu.VMEM((2, scans, scans), jnp.bfloat16),
            pltpu.VMEM((rows, scans), jnp.float32),
            pltpu.VMEM((rows, scans), jnp.float32),
        ],
    )
    return pl.pallas_call(
        wavelet_kernel,
        grid_spec=grid_spec,
        out_shape=[
            jax.ShapeDtypeStruct((frames, strip, scans), jnp.bfloat16),
            jax.ShapeDtypeStruct((frames, strip, scans), jnp.float32),
        ],
        compiler_params=pltpu.CompilerParams(
            dimension_semantics=("arbitrary",), vmem_limit_bytes=56 * 1024 * 1024
        ),
        interpret=interpret,
    )(first, ftab, low, slab, high, blocks)


def compute(slab, block_index, low, high, widths, interpret=False):
    frames, strip, scans = low.shape
    depth = -(-(frames + 2 * HALO) // TILE) * TILE
    scale_widths = widths.astype(jnp.float32)
    ftab = frame_tables(frames, scale_widths, depth)
    blocks = scan_blocks(scans, scale_widths)
    first = jnp.reshape(block_index, (1,)).astype(jnp.int32)
    return wavelet_core(first, ftab, low, slab, high, blocks, interpret)


def per_device(slab, widths):
    strip = slab.shape[1] // lax.axis_size("scale")
    low, high = halos(slab, strip)
    return compute(slab, lax.axis_index("scale"), low, high, widths)


def solution(mesh):
    in_specs = (P("rt", None, None), P())
    out_specs = (P("rt", "scale", None), P("rt", "scale", None))
    return jax.shard_map(
        per_device, mesh=mesh, in_specs=in_specs, out_specs=out_specs, check_vma=False
    )
```

```python
import jax
import jax.numpy as jnp
from jax import lax
from jax.experimental import pallas as pl
from jax.experimental.pallas import tpu as pltpu
from jax.sharding import PartitionSpec as P

SCAN_RATIO = 16
HALO = 24
TILE = 128


def mexican(offsets, spread):
    ratio = offsets / spread
    return (1.0 - ratio * ratio) * jnp.exp(-0.5 * ratio * ratio) / jnp.sqrt(spread)


def halos(slab, strip):
    n_scale, n_rt = lax.axis_size("scale"), lax.axis_size("rt")
    half = n_scale // 2
    s, r = lax.axis_index("scale"), lax.axis_index("rt")
    other = (s + half) % n_scale
    forward, backward = [], []
    for ss in range(n_scale):
        for rr in range(n_rt):
            flip = (ss + half) % n_scale
            if rr + 1 < n_rt:
                forward.append((ss * n_rt + rr, (ss if rr % 2 == 0 else flip) * n_rt + rr + 1))
            if rr > 0:
                backward.append((ss * n_rt + rr, (ss if rr % 2 == 1 else flip) * n_rt + rr - 1))
    frames = slab.shape[0]

    def piece(index, start):
        part = lax.dynamic_slice_in_dim(slab, index * strip, strip, axis=1)
        part = lax.slice_in_dim(part, start, start + HALO, axis=0)
        return part.astype(jnp.bfloat16)

    send_fwd = piece(jnp.where(r % 2 == 0, s, other), frames - HALO)
    send_bwd = piece(jnp.where(r % 2 == 1, s, other), 0)
    low = lax.ppermute(send_fwd, ("scale", "rt"), forward)
    high = lax.ppermute(send_bwd, ("scale", "rt"), backward)
    return low, high


def frame_tables(frames, scale_widths, depth):
    out_pos = jnp.arange(frames, dtype=jnp.float32)
    in_pos = jnp.arange(depth, dtype=jnp.float32) - HALO
    offsets = (in_pos[None, :] - out_pos[:, None])[None]
    spread = scale_widths[:, None, None]
    inside = (jnp.abs(offsets) <= HALO) & (in_pos < frames + HALO)[None, None, :]
    values = jnp.where(inside, mexican(offsets, spread), 0.0)
    return values.astype(jnp.bfloat16).reshape(-1, depth)


def scan_blocks(scans, scale_widths):
    nb = scans // TILE
    shift = (jnp.arange(2 * nb - 1, dtype=jnp.float32) - (nb - 1)) * TILE
    pos = jnp.arange(TILE, dtype=jnp.float32)
    offsets = shift[:, None, None] + (pos[:, None] - pos[None, :])[None]
    spread = SCAN_RATIO * scale_widths[:, None, None, None]
    return mexican(offsets[None], spread).astype(jnp.bfloat16)


def wavelet_kernel(strip_ref, f_ref, lo_hbm, own_ref, hi_hbm, b_hbm, peak_ref, energy_ref,
                   lo_buf, hi_buf, b_buf, sem, p_scr, g_scr, s_scr, best_scr, total_scr):
    count, rows, scans = g_scr.shape
    frames, strip, _ = own_ref.shape
    nb = scans // TILE
    used = 2 * HALO + frames

    def table_copy(c):
        return pltpu.make_async_copy(b_hbm.at[c], b_buf.at[c % 2], sem.at[c % 2])

    lo_copy = pltpu.make_async_copy(lo_hbm, lo_buf, sem.at[2])
    hi_copy = pltpu.make_async_copy(hi_hbm, hi_buf, sem.at[3])
    lo_copy.start()
    hi_copy.start()
    table_copy(0).start()
    table_copy(1).start()

    p_scr[used:, :] = jnp.zeros((p_scr.shape[0] - used, p_scr.shape[1]), p_scr.dtype)
    for m in range(strip):
        cols = slice(m * scans, (m + 1) * scans)
        p_scr[HALO:HALO + frames, cols] = own_ref[:, m, :]
    lo_copy.wait()
    hi_copy.wait()
    for m in range(strip):
        cols = slice(m * scans, (m + 1) * scans)
        p_scr[0:HALO, cols] = lo_buf[:, m, :].astype(jnp.float32)
        p_scr[HALO + frames:used, cols] = hi_buf[:, m, :].astype(jnp.float32)
    fall = f_ref[...]
    for m in range(strip):
        part = p_scr[:, m * scans:(m + 1) * scans].astype(jnp.bfloat16)
        gm = jnp.dot(fall, part, preferred_element_type=jnp.float32)
        for cc in range(count):
            g_scr[cc, m * frames:(m + 1) * frames, :] = gm[cc * frames:(cc + 1) * frames, :]

    for c in range(count):
        table = s_scr.at[c % 2]
        blocks = b_buf.at[c % 2]
        table_copy(c).wait()
        for i in range(nb):
            for j in range(nb):
                table[i * TILE:(i + 1) * TILE, j * TILE:(j + 1) * TILE] = blocks[i - j + nb - 1]
        if c + 2 < count:
            table_copy(c + 2).start()
        lhs = g_scr[c].astype(jnp.bfloat16)
        answer = jnp.dot(lhs, table[...], preferred_element_type=jnp.float32).astype(jnp.bfloat16)
        answer = answer.astype(jnp.float32)
        if c == 0:
            best_scr[...] = answer
            total_scr[...] = answer * answer
        else:
            best_scr[...] = jnp.maximum(best_scr[...], answer)
            total_scr[...] = total_scr[...] + answer * answer

    for m in range(strip):
        peak_ref[:, m, :] = best_scr[m * frames:(m + 1) * frames, :].astype(peak_ref.dtype)
        energy_ref[:, m, :] = total_scr[m * frames:(m + 1) * frames, :]


def wavelet_core(first, ftab, low, slab, high, blocks, interpret=False):
    count = blocks.shape[0]
    depth = ftab.shape[1]
    frames, strip, scans = low.shape
    rows = frames * strip
    nblk = blocks.shape[1]
    whole = lambda c, i: (0, 0)
    whole3 = lambda c, i: (0, 0, 0)
    grid_spec = pltpu.PrefetchScalarGridSpec(
        num_scalar_prefetch=1,
        grid=(1,),
        in_specs=[
            pl.BlockSpec((count * frames, depth), whole),
            pl.BlockSpec(memory_space=pl.ANY),
            pl.BlockSpec((frames, strip, scans), lambda c, i: (0, i[0], 0)),
            pl.BlockSpec(memory_space=pl.ANY),
            pl.BlockSpec(memory_space=pl.ANY),
        ],
        out_specs=[
            pl.BlockSpec((frames, strip, scans), whole3),
            pl.BlockSpec((frames, strip, scans), whole3),
        ],
        scratch_shapes=[
            pltpu.VMEM((HALO, strip, scans), low.dtype),
            pltpu.VMEM((HALO, strip, scans), high.dtype),
            pltpu.VMEM((2, nblk, TILE, TILE), blocks.dtype),
            pltpu.SemaphoreType.DMA((4,)),
            pltpu.VMEM((depth, strip * scans), jnp.float32),
            pltpu.VMEM((count, rows, scans), jnp.float32),
            pltpu.VMEM((2, scans, scans), jnp.bfloat16),
            pltpu.VMEM((rows, scans), jnp.float32),
            pltpu.VMEM((rows, scans), jnp.float32),
        ],
    )
    return pl.pallas_call(
        wavelet_kernel,
        grid_spec=grid_spec,
        out_shape=[
            jax.ShapeDtypeStruct((frames, strip, scans), jnp.bfloat16),
            jax.ShapeDtypeStruct((frames, strip, scans), jnp.float32),
        ],
        compiler_params=pltpu.CompilerParams(
            dimension_semantics=("arbitrary",), vmem_limit_bytes=56 * 1024 * 1024
        ),
        interpret=interpret,
    )(first, ftab, low, slab, high, blocks)


def compute(slab, block_index, low, high, widths, interpret=False):
    frames, strip, scans = low.shape
    depth = -(-(frames + 2 * HALO) // TILE) * TILE
    scale_widths = widths.astype(jnp.float32)
    ftab = frame_tables(frames, scale_widths, depth)
    blocks = scan_blocks(scans, scale_widths)
    first = jnp.reshape(block_index, (1,)).astype(jnp.int32)
    return wavelet_core(first, ftab, low, slab, high, blocks, interpret)


def per_device(slab, widths):
    strip = slab.shape[1] // lax.axis_size("scale")
    low, high = halos(slab, strip)
    return compute(slab, lax.axis_index("scale"), low, high, widths)


def solution(mesh):
    in_specs = (P("rt", None, None), P())
    out_specs = (P("rt", "scale", None), P("rt", "scale", None))
    return jax.shard_map(
        per_device, mesh=mesh, in_specs=in_specs, out_specs=out_specs, check_vma=False
    )
```

```python
import jax
import jax.numpy as jnp
from jax import lax
from jax.experimental import pallas as pl
from jax.experimental.pallas import tpu as pltpu
from jax.sharding import PartitionSpec as P

SCAN_RATIO = 16
HALO = 24
TILE = 128
STEPS = 2


def mexican(offsets, spread):
    ratio = offsets / spread
    return (1.0 - ratio * ratio) * jnp.exp(-0.5 * ratio * ratio) / jnp.sqrt(spread)


def halos(slab, strip):
    n_scale, n_rt = lax.axis_size("scale"), lax.axis_size("rt")
    half = n_scale // 2
    s, r = lax.axis_index("scale"), lax.axis_index("rt")
    other = (s + half) % n_scale
    forward, backward = [], []
    for ss in range(n_scale):
        for rr in range(n_rt):
            flip = (ss + half) % n_scale
            if rr + 1 < n_rt:
                forward.append((ss * n_rt + rr, (ss if rr % 2 == 0 else flip) * n_rt + rr + 1))
            if rr > 0:
                backward.append((ss * n_rt + rr, (ss if rr % 2 == 1 else flip) * n_rt + rr - 1))
    frames = slab.shape[0]

    def piece(index, start):
        part = lax.dynamic_slice_in_dim(slab, index * strip, strip, axis=1)
        part = lax.slice_in_dim(part, start, start + HALO, axis=0)
        return part.astype(jnp.bfloat16)

    send_fwd = piece(jnp.where(r % 2 == 0, s, other), frames - HALO)
    send_bwd = piece(jnp.where(r % 2 == 1, s, other), 0)
    low = lax.ppermute(send_fwd, ("scale", "rt"), forward)
    high = lax.ppermute(send_bwd, ("scale", "rt"), backward)
    return low, high


def frame_tables(frames, scale_widths, depth):
    out_pos = jnp.arange(frames, dtype=jnp.float32)
    in_pos = jnp.arange(depth, dtype=jnp.float32) - HALO
    offsets = (in_pos[None, :] - out_pos[:, None])[None]
    spread = scale_widths[:, None, None]
    inside = (jnp.abs(offsets) <= HALO) & (in_pos < frames + HALO)[None, None, :]
    values = jnp.where(inside, mexican(offsets, spread), 0.0)
    return values.astype(jnp.bfloat16).reshape(-1, depth)


def scan_blocks(scans, scale_widths):
    nb = scans // TILE
    shift = (jnp.arange(2 * nb - 1, dtype=jnp.float32) - (nb - 1)) * TILE
    pos = jnp.arange(TILE, dtype=jnp.float32)
    offsets = shift[:, None, None] + (pos[:, None] - pos[None, :])[None]
    spread = SCAN_RATIO * scale_widths[:, None, None, None]
    return mexican(offsets[None], spread).astype(jnp.bfloat16)


def wavelet_kernel(strip_ref, f_ref, lo_ref, own_ref, hi_ref, b_ref, peak_ref, energy_ref,
                   p_scr, g_scr, s_scr, best_scr, total_scr):
    step = pl.program_id(0)
    count, rows, scans = g_scr.shape
    per = b_ref.shape[0]
    frames, strip, _ = own_ref.shape
    nb = scans // TILE
    used = 2 * HALO + frames

    @pl.when(step == 0)
    def _():
        p_scr[used:, :] = jnp.zeros((p_scr.shape[0] - used, p_scr.shape[1]), p_scr.dtype)
        for m in range(strip):
            cols = slice(m * scans, (m + 1) * scans)
            p_scr[0:HALO, cols] = lo_ref[:, m, :].astype(jnp.float32)
            p_scr[HALO:HALO + frames, cols] = own_ref[:, m, :]
            p_scr[HALO + frames:used, cols] = hi_ref[:, m, :].astype(jnp.float32)
        fall = f_ref[...]
        for m in range(strip):
            part = p_scr[:, m * scans:(m + 1) * scans].astype(jnp.bfloat16)
            gm = jnp.dot(fall, part, preferred_element_type=jnp.float32)
            for cc in range(count):
                g_scr[cc, m * frames:(m + 1) * frames, :] = gm[cc * frames:(cc + 1) * frames, :]
        best_scr[...] = jnp.full(best_scr.shape, -jnp.inf, best_scr.dtype)
        total_scr[...] = jnp.zeros(total_scr.shape, total_scr.dtype)

    for k in range(per):
        table = s_scr.at[k % 2]
        for i in range(nb):
            for j in range(nb):
                table[i * TILE:(i + 1) * TILE, j * TILE:(j + 1) * TILE] = b_ref[k, i - j + nb - 1]
        lhs = g_scr[step * per + k].astype(jnp.bfloat16)
        answer = jnp.dot(lhs, table[...], preferred_element_type=jnp.float32).astype(jnp.bfloat16)
        answer = answer.astype(jnp.float32)
        best_scr[...] = jnp.maximum(best_scr[...], answer)
        total_scr[...] = total_scr[...] + answer * answer

    @pl.when(step == pl.num_programs(0) - 1)
    def _():
        for m in range(strip):
            peak_ref[:, m, :] = best_scr[m * frames:(m + 1) * frames, :].astype(peak_ref.dtype)
            energy_ref[:, m, :] = total_scr[m * frames:(m + 1) * frames, :]


def wavelet_core(first, ftab, low, slab, high, blocks, interpret=False):
    count = blocks.shape[0]
    depth = ftab.shape[1]
    frames, strip, scans = low.shape
    rows = frames * strip
    nblk = blocks.shape[1]
    whole = lambda c, i: (0, 0)
    whole3 = lambda c, i: (0, 0, 0)
    grid_spec = pltpu.PrefetchScalarGridSpec(
        num_scalar_prefetch=1,
        grid=(STEPS,),
        in_specs=[
            pl.BlockSpec((count * frames, depth), whole),
            pl.BlockSpec((HALO, strip, scans), whole3),
            pl.BlockSpec((frames, strip, scans), lambda c, i: (0, i[0], 0)),
            pl.BlockSpec((HALO, strip, scans), whole3),
            pl.BlockSpec((count // STEPS, nblk, TILE, TILE), lambda c, i: (c, 0, 0, 0)),
        ],
        out_specs=[
            pl.BlockSpec((frames, strip, scans), whole3),
            pl.BlockSpec((frames, strip, scans), whole3),
        ],
        scratch_shapes=[
            pltpu.VMEM((depth, strip * scans), jnp.float32),
            pltpu.VMEM((count, rows, scans), jnp.float32),
            pltpu.VMEM((2, scans, scans), jnp.bfloat16),
            pltpu.VMEM((rows, scans), jnp.float32),
            pltpu.VMEM((rows, scans), jnp.float32),
        ],
    )
    return pl.pallas_call(
        wavelet_kernel,
        grid_spec=grid_spec,
        out_shape=[
            jax.ShapeDtypeStruct((frames, strip, scans), jnp.bfloat16),
            jax.ShapeDtypeStruct((frames, strip, scans), jnp.float32),
        ],
        compiler_params=pltpu.CompilerParams(
            dimension_semantics=("arbitrary",), vmem_limit_bytes=56 * 1024 * 1024
        ),
        interpret=interpret,
    )(first, ftab, low, slab, high, blocks)


def compute(slab, block_index, low, high, widths, interpret=False):
    frames, strip, scans = low.shape
    depth = -(-(frames + 2 * HALO) // TILE) * TILE
    scale_widths = widths.astype(jnp.float32)
    ftab = frame_tables(frames, scale_widths, depth)
    blocks = scan_blocks(scans, scale_widths)
    first = jnp.reshape(block_index, (1,)).astype(jnp.int32)
    return wavelet_core(first, ftab, low, slab, high, blocks, interpret)


def per_device(slab, widths):
    strip = slab.shape[1] // lax.axis_size("scale")
    low, high = halos(slab, strip)
    return compute(slab, lax.axis_index("scale"), low, high, widths)


def solution(mesh):
    in_specs = (P("rt", None, None), P())
    out_specs = (P("rt", "scale", None), P("rt", "scale", None))
    return jax.shard_map(
        per_device, mesh=mesh, in_specs=in_specs, out_specs=out_specs, check_vma=False
    )
```

```python
import jax
import jax.numpy as jnp
from jax import lax
from jax.experimental import pallas as pl
from jax.experimental.pallas import tpu as pltpu
from jax.sharding import PartitionSpec as P

SCAN_RATIO = 16
HALO = 24
TILE = 128


def mexican(offsets, spread):
    ratio = offsets / spread
    return (1.0 - ratio * ratio) * jnp.exp(-0.5 * ratio * ratio) / jnp.sqrt(spread)


def halos(slab, strip):
    n_scale, n_rt = lax.axis_size("scale"), lax.axis_size("rt")
    half = n_scale // 2
    s, r = lax.axis_index("scale"), lax.axis_index("rt")
    other = (s + half) % n_scale
    forward, backward = [], []
    for ss in range(n_scale):
        for rr in range(n_rt):
            flip = (ss + half) % n_scale
            if rr + 1 < n_rt:
                forward.append((ss * n_rt + rr, (ss if rr % 2 == 0 else flip) * n_rt + rr + 1))
            if rr > 0:
                backward.append((ss * n_rt + rr, (ss if rr % 2 == 1 else flip) * n_rt + rr - 1))
    frames = slab.shape[0]

    def piece(index, start):
        part = lax.dynamic_slice_in_dim(slab, index * strip, strip, axis=1)
        part = lax.slice_in_dim(part, start, start + HALO, axis=0)
        return part.astype(jnp.bfloat16)

    send_fwd = piece(jnp.where(r % 2 == 0, s, other), frames - HALO)
    send_bwd = piece(jnp.where(r % 2 == 1, s, other), 0)
    low = lax.ppermute(send_fwd, ("scale", "rt"), forward)
    high = lax.ppermute(send_bwd, ("scale", "rt"), backward)
    return low, high


def frame_tables(frames, scale_widths, depth):
    out_pos = jnp.arange(frames, dtype=jnp.float32)
    in_pos = jnp.arange(depth, dtype=jnp.float32) - HALO
    offsets = (in_pos[None, :] - out_pos[:, None])[None]
    spread = scale_widths[:, None, None]
    inside = (jnp.abs(offsets) <= HALO) & (in_pos < frames + HALO)[None, None, :]
    values = jnp.where(inside, mexican(offsets, spread), 0.0)
    return values.astype(jnp.bfloat16).reshape(-1, depth)


def scan_blocks(scans, scale_widths):
    nb = scans // TILE
    shift = (jnp.arange(2 * nb - 1, dtype=jnp.float32) - (nb - 1)) * TILE
    pos = jnp.arange(TILE, dtype=jnp.float32)
    offsets = shift[:, None, None] + (pos[:, None] - pos[None, :])[None]
    spread = SCAN_RATIO * scale_widths[:, None, None, None]
    return mexican(offsets[None], spread).astype(jnp.bfloat16)


def wavelet_kernel(strip_ref, f_ref, lo_ref, own_ref, hi_ref, b_ref, late_hbm, peak_ref, energy_ref,
                   late_buf, sem, p_scr, g_scr, s_scr, best_scr, total_scr):
    count, rows, scans = g_scr.shape
    frames, strip, _ = own_ref.shape
    nb = scans // TILE
    used = 2 * HALO + frames
    early = b_ref.shape[0]
    late_copy = pltpu.make_async_copy(late_hbm, late_buf, sem.at[0])
    late_copy.start()

    p_scr[used:, :] = jnp.zeros((p_scr.shape[0] - used, p_scr.shape[1]), p_scr.dtype)
    for m in range(strip):
        cols = slice(m * scans, (m + 1) * scans)
        p_scr[0:HALO, cols] = lo_ref[:, m, :].astype(jnp.float32)
        p_scr[HALO:HALO + frames, cols] = own_ref[:, m, :]
        p_scr[HALO + frames:used, cols] = hi_ref[:, m, :].astype(jnp.float32)
    fall = f_ref[...]
    for m in range(strip):
        part = p_scr[:, m * scans:(m + 1) * scans].astype(jnp.bfloat16)
        gm = jnp.dot(fall, part, preferred_element_type=jnp.float32)
        for cc in range(count):
            g_scr[cc, m * frames:(m + 1) * frames, :] = gm[cc * frames:(cc + 1) * frames, :]

    for c in range(count):
        table = s_scr.at[c % 2]
        if c == early:
            late_copy.wait()
        blocks = b_ref.at[c] if c < early else late_buf.at[c - early]
        for i in range(nb):
            for j in range(nb):
                table[i * TILE:(i + 1) * TILE, j * TILE:(j + 1) * TILE] = blocks[i - j + nb - 1]
        lhs = g_scr[c].astype(jnp.bfloat16)
        answer = jnp.dot(lhs, table[...], preferred_element_type=jnp.float32).astype(jnp.bfloat16)
        answer = answer.astype(jnp.float32)
        if c == 0:
            best_scr[...] = answer
            total_scr[...] = answer * answer
        else:
            best_scr[...] = jnp.maximum(best_scr[...], answer)
            total_scr[...] = total_scr[...] + answer * answer

    for m in range(strip):
        peak_ref[:, m, :] = best_scr[m * frames:(m + 1) * frames, :].astype(peak_ref.dtype)
        energy_ref[:, m, :] = total_scr[m * frames:(m + 1) * frames, :]


def wavelet_core(first, ftab, low, slab, high, blocks, interpret=False):
    count = blocks.shape[0]
    depth = ftab.shape[1]
    frames, strip, scans = low.shape
    rows = frames * strip
    nblk = blocks.shape[1]
    whole = lambda c, i: (0, 0)
    whole3 = lambda c, i: (0, 0, 0)
    grid_spec = pltpu.PrefetchScalarGridSpec(
        num_scalar_prefetch=1,
        grid=(1,),
        in_specs=[
            pl.BlockSpec((count * frames, depth), whole),
            pl.BlockSpec((HALO, strip, scans), whole3),
            pl.BlockSpec((frames, strip, scans), lambda c, i: (0, i[0], 0)),
            pl.BlockSpec((HALO, strip, scans), whole3),
            pl.BlockSpec((count // 2, nblk, TILE, TILE), lambda c, i: (0, 0, 0, 0)),
            pl.BlockSpec(memory_space=pl.ANY),
        ],
        out_specs=[
            pl.BlockSpec((frames, strip, scans), whole3),
            pl.BlockSpec((frames, strip, scans), whole3),
        ],
        scratch_shapes=[
            pltpu.VMEM((count - count // 2, nblk, TILE, TILE), blocks.dtype),
            pltpu.SemaphoreType.DMA((1,)),
            pltpu.VMEM((depth, strip * scans), jnp.float32),
            pltpu.VMEM((count, rows, scans), jnp.float32),
            pltpu.VMEM((2, scans, scans), jnp.bfloat16),
            pltpu.VMEM((rows, scans), jnp.float32),
            pltpu.VMEM((rows, scans), jnp.float32),
        ],
    )
    return pl.pallas_call(
        wavelet_kernel,
        grid_spec=grid_spec,
        out_shape=[
            jax.ShapeDtypeStruct((frames, strip, scans), jnp.bfloat16),
            jax.ShapeDtypeStruct((frames, strip, scans), jnp.float32),
        ],
        compiler_params=pltpu.CompilerParams(
            dimension_semantics=("arbitrary",), vmem_limit_bytes=56 * 1024 * 1024
        ),
        interpret=interpret,
    )(first, ftab, low, slab, high, blocks[:count // 2], blocks[count // 2:])


def compute(slab, block_index, low, high, widths, interpret=False):
    frames, strip, scans = low.shape
    depth = -(-(frames + 2 * HALO) // TILE) * TILE
    scale_widths = widths.astype(jnp.float32)
    ftab = frame_tables(frames, scale_widths, depth)
    blocks = scan_blocks(scans, scale_widths)
    first = jnp.reshape(block_index, (1,)).astype(jnp.int32)
    return wavelet_core(first, ftab, low, slab, high, blocks, interpret)


def per_device(slab, widths):
    strip = slab.shape[1] // lax.axis_size("scale")
    low, high = halos(slab, strip)
    return compute(slab, lax.axis_index("scale"), low, high, widths)


def solution(mesh):
    in_specs = (P("rt", None, None), P())
    out_specs = (P("rt", "scale", None), P("rt", "scale", None))
    return jax.shard_map(
        per_device, mesh=mesh, in_specs=in_specs, out_specs=out_specs, check_vma=False
    )
```

```python
import jax
import jax.numpy as jnp
from jax import lax
from jax.experimental import pallas as pl
from jax.experimental.pallas import tpu as pltpu
from jax.sharding import PartitionSpec as P

SCAN_RATIO = 16
HALO = 24
TILE = 128
SLOT = 32


def mexican(offsets, spread):
    ratio = offsets / spread
    return (1.0 - ratio * ratio) * jnp.exp(-0.5 * ratio * ratio) / jnp.sqrt(spread)


def halos(slab, strip):
    n_scale, n_rt = lax.axis_size("scale"), lax.axis_size("rt")
    half = n_scale // 2
    s, r = lax.axis_index("scale"), lax.axis_index("rt")
    other = (s + half) % n_scale
    forward, backward = [], []
    for ss in range(n_scale):
        for rr in range(n_rt):
            flip = (ss + half) % n_scale
            if rr + 1 < n_rt:
                forward.append((ss * n_rt + rr, (ss if rr % 2 == 0 else flip) * n_rt + rr + 1))
            if rr > 0:
                backward.append((ss * n_rt + rr, (ss if rr % 2 == 1 else flip) * n_rt + rr - 1))
    frames = slab.shape[0]

    def piece(index, start):
        part = lax.dynamic_slice_in_dim(slab, index * strip, strip, axis=1)
        part = lax.slice_in_dim(part, start, start + HALO, axis=0)
        return part.astype(jnp.bfloat16)

    send_fwd = piece(jnp.where(r % 2 == 0, s, other), frames - HALO)
    send_bwd = piece(jnp.where(r % 2 == 1, s, other), 0)
    low = lax.ppermute(send_fwd, ("scale", "rt"), forward)
    high = lax.ppermute(send_bwd, ("scale", "rt"), backward)
    return low, high


def frame_tables(frames, scale_widths, depth, slot):
    out_pos = jnp.arange(frames, dtype=jnp.float32)
    k = jnp.arange(depth)
    piece, rest = k // slot, k % slot
    size = jnp.where(piece == 1, frames, HALO)
    valid = (piece < 3) & (rest < size)
    in_pos = jnp.where(piece == 0, rest - HALO, jnp.where(piece == 1, rest, frames + rest)).astype(jnp.float32)
    offsets = (in_pos[None, :] - out_pos[:, None])[None]
    spread = scale_widths[:, None, None]
    inside = (jnp.abs(offsets) <= HALO) & valid[None, None, :]
    values = jnp.where(inside, mexican(offsets, spread), 0.0)
    return values.astype(jnp.bfloat16).reshape(-1, depth)


def scan_blocks(scans, scale_widths):
    nb = scans // TILE
    shift = (jnp.arange(2 * nb - 1, dtype=jnp.float32) - (nb - 1)) * TILE
    pos = jnp.arange(TILE, dtype=jnp.float32)
    offsets = shift[:, None, None] + (pos[:, None] - pos[None, :])[None]
    spread = SCAN_RATIO * scale_widths[:, None, None, None]
    return mexican(offsets[None], spread).astype(jnp.bfloat16)


def wavelet_kernel(strip_ref, f_ref, lo_ref, own_ref, hi_ref, b_ref, peak_ref, energy_ref,
                   p_scr, g_scr, s_scr, best_scr, total_scr):
    count, rows, scans = g_scr.shape
    frames, strip, _ = own_ref.shape
    nb = scans // TILE
    slot = SLOT

    p_scr[...] = jnp.zeros(p_scr.shape, p_scr.dtype)
    for m in range(strip):
        cols = slice(m * scans, (m + 1) * scans)
        p_scr[0:HALO, cols] = lo_ref[:, m, :]
        p_scr[slot:slot + frames, cols] = own_ref[:, m, :].astype(p_scr.dtype)
        p_scr[2 * slot:2 * slot + HALO, cols] = hi_ref[:, m, :]
    fall = f_ref[...]
    for m in range(strip):
        part = p_scr[:, m * scans:(m + 1) * scans]
        gm = jnp.dot(fall, part, preferred_element_type=jnp.float32)
        for cc in range(count):
            g_scr[cc, m * frames:(m + 1) * frames, :] = gm[cc * frames:(cc + 1) * frames, :]

    for c in range(count):
        table = s_scr.at[c % 2]
        for i in range(nb):
            for j in range(nb):
                table[i * TILE:(i + 1) * TILE, j * TILE:(j + 1) * TILE] = b_ref[c, i - j + nb - 1]
        lhs = g_scr[c].astype(jnp.bfloat16)
        answer = jnp.dot(lhs, table[...], preferred_element_type=jnp.float32).astype(jnp.bfloat16)
        answer = answer.astype(jnp.float32)
        if c == 0:
            best_scr[...] = answer
            total_scr[...] = answer * answer
        else:
            best_scr[...] = jnp.maximum(best_scr[...], answer)
            total_scr[...] = total_scr[...] + answer * answer

    for m in range(strip):
        peak_ref[:, m, :] = best_scr[m * frames:(m + 1) * frames, :].astype(peak_ref.dtype)
        energy_ref[:, m, :] = total_scr[m * frames:(m + 1) * frames, :]


def wavelet_core(first, ftab, low, slab, high, blocks, interpret=False):
    count = blocks.shape[0]
    depth = ftab.shape[1]
    frames, strip, scans = low.shape
    rows = frames * strip
    nblk = blocks.shape[1]
    whole = lambda c, i: (0, 0)
    whole3 = lambda c, i: (0, 0, 0)
    grid_spec = pltpu.PrefetchScalarGridSpec(
        num_scalar_prefetch=1,
        grid=(1,),
        in_specs=[
            pl.BlockSpec((count * frames, depth), whole),
            pl.BlockSpec((HALO, strip, scans), whole3),
            pl.BlockSpec((frames, strip, scans), lambda c, i: (0, i[0], 0)),
            pl.BlockSpec((HALO, strip, scans), whole3),
            pl.BlockSpec((count, nblk, TILE, TILE), lambda c, i: (0, 0, 0, 0)),
        ],
        out_specs=[
            pl.BlockSpec((frames, strip, scans), whole3),
            pl.BlockSpec((frames, strip, scans), whole3),
        ],
        scratch_shapes=[
            pltpu.VMEM((depth, strip * scans), jnp.bfloat16),
            pltpu.VMEM((count, rows, scans), jnp.float32),
            pltpu.VMEM((2, scans, scans), jnp.bfloat16),
            pltpu.VMEM((rows, scans), jnp.float32),
            pltpu.VMEM((rows, scans), jnp.float32),
        ],
    )
    return pl.pallas_call(
        wavelet_kernel,
        grid_spec=grid_spec,
        out_shape=[
            jax.ShapeDtypeStruct((frames, strip, scans), jnp.bfloat16),
            jax.ShapeDtypeStruct((frames, strip, scans), jnp.float32),
        ],
        compiler_params=pltpu.CompilerParams(
            dimension_semantics=("arbitrary",), vmem_limit_bytes=56 * 1024 * 1024
        ),
        interpret=interpret,
    )(first, ftab, low, slab, high, blocks)


def compute(slab, block_index, low, high, widths, interpret=False):
    frames, strip, scans = low.shape
    assert max(HALO, frames) <= SLOT
    depth = -(-(3 * SLOT) // TILE) * TILE
    scale_widths = widths.astype(jnp.float32)
    ftab = frame_tables(frames, scale_widths, depth, SLOT)
    blocks = scan_blocks(scans, scale_widths)
    first = jnp.reshape(block_index, (1,)).astype(jnp.int32)
    return wavelet_core(first, ftab, low, slab, high, blocks, interpret)


def per_device(slab, widths):
    strip = slab.shape[1] // lax.axis_size("scale")
    low, high = halos(slab, strip)
    return compute(slab, lax.axis_index("scale"), low, high, widths)


def solution(mesh):
    in_specs = (P("rt", None, None), P())
    out_specs = (P("rt", "scale", None), P("rt", "scale", None))
    return jax.shard_map(
        per_device, mesh=mesh, in_specs=in_specs, out_specs=out_specs, check_vma=False
    )
```

```python
import jax
import jax.numpy as jnp
from jax import lax
from jax.experimental import pallas as pl
from jax.experimental.pallas import tpu as pltpu
from jax.sharding import PartitionSpec as P

SCAN_RATIO = 16
HALO = 24
TILE = 128


def mexican(offsets, spread):
    ratio = offsets / spread
    return (1.0 - ratio * ratio) * jnp.exp(-0.5 * ratio * ratio) / jnp.sqrt(spread)


def halos(slab, strip):
    n_scale, n_rt = lax.axis_size("scale"), lax.axis_size("rt")
    half = n_scale // 2
    s, r = lax.axis_index("scale"), lax.axis_index("rt")
    other = (s + half) % n_scale
    forward, backward = [], []
    for ss in range(n_scale):
        for rr in range(n_rt):
            flip = (ss + half) % n_scale
            if rr + 1 < n_rt:
                forward.append((ss * n_rt + rr, (ss if rr % 2 == 0 else flip) * n_rt + rr + 1))
            if rr > 0:
                backward.append((ss * n_rt + rr, (ss if rr % 2 == 1 else flip) * n_rt + rr - 1))
    frames = slab.shape[0]

    def piece(index, start):
        part = lax.dynamic_slice_in_dim(slab, index * strip, strip, axis=1)
        part = lax.slice_in_dim(part, start, start + HALO, axis=0)
        return part.astype(jnp.bfloat16)

    send_fwd = piece(jnp.where(r % 2 == 0, s, other), frames - HALO)
    send_bwd = piece(jnp.where(r % 2 == 1, s, other), 0)
    low = lax.ppermute(send_fwd, ("scale", "rt"), forward)
    high = lax.ppermute(send_bwd, ("scale", "rt"), backward)
    return low, high


def frame_tables(frames, scale_widths, depth):
    out_pos = jnp.arange(frames, dtype=jnp.float32)
    in_pos = jnp.arange(depth, dtype=jnp.float32) - HALO
    offsets = (in_pos[None, :] - out_pos[:, None])[None]
    spread = scale_widths[:, None, None]
    inside = (jnp.abs(offsets) <= HALO) & (in_pos < frames + HALO)[None, None, :]
    values = jnp.where(inside, mexican(offsets, spread), 0.0)
    return values.astype(jnp.bfloat16).reshape(-1, depth)


def scan_blocks(scans, scale_widths):
    nb = scans // TILE
    shift = jnp.arange(nb, dtype=jnp.float32) * TILE
    pos = jnp.arange(TILE, dtype=jnp.float32)
    offsets = shift[:, None, None] + (pos[:, None] - pos[None, :])[None]
    spread = SCAN_RATIO * scale_widths[:, None, None, None]
    return mexican(offsets[None], spread).astype(jnp.bfloat16)


def wavelet_kernel(strip_ref, f_ref, lo_ref, own_ref, hi_ref, b_ref, peak_ref, energy_ref,
                   p_scr, g_scr, s_scr, best_scr, total_scr):
    count, rows, scans = g_scr.shape
    frames, strip, _ = own_ref.shape
    nb = scans // TILE
    used = 2 * HALO + frames

    p_scr[used:, :] = jnp.zeros((p_scr.shape[0] - used, p_scr.shape[1]), p_scr.dtype)
    for m in range(strip):
        cols = slice(m * scans, (m + 1) * scans)
        p_scr[0:HALO, cols] = lo_ref[:, m, :].astype(jnp.float32)
        p_scr[HALO:HALO + frames, cols] = own_ref[:, m, :]
        p_scr[HALO + frames:used, cols] = hi_ref[:, m, :].astype(jnp.float32)
    fall = f_ref[...]
    for m in range(strip):
        part = p_scr[:, m * scans:(m + 1) * scans].astype(jnp.bfloat16)
        gm = jnp.dot(fall, part, preferred_element_type=jnp.float32)
        for cc in range(count):
            g_scr[cc, m * frames:(m + 1) * frames, :] = gm[cc * frames:(cc + 1) * frames, :]

    for c in range(count):
        table = s_scr.at[c % 2]
        flipped = {d: b_ref[c, d].T for d in range(1, nb)}
        for i in range(nb):
            for j in range(nb):
                block = b_ref[c, i - j] if i >= j else flipped[j - i]
                table[i * TILE:(i + 1) * TILE, j * TILE:(j + 1) * TILE] = block
        lhs = g_scr[c].astype(jnp.bfloat16)
        answer = jnp.dot(lhs, table[...], preferred_element_type=jnp.float32).astype(jnp.bfloat16)
        answer = answer.astype(jnp.float32)
        if c == 0:
            best_scr[...] = answer
            total_scr[...] = answer * answer
        else:
            best_scr[...] = jnp.maximum(best_scr[...], answer)
            total_scr[...] = total_scr[...] + answer * answer

    for m in range(strip):
        peak_ref[:, m, :] = best_scr[m * frames:(m + 1) * frames, :].astype(peak_ref.dtype)
        energy_ref[:, m, :] = total_scr[m * frames:(m + 1) * frames, :]


def wavelet_core(first, ftab, low, slab, high, blocks, interpret=False):
    count = blocks.shape[0]
    depth = ftab.shape[1]
    frames, strip, scans = low.shape
    rows = frames * strip
    nblk = blocks.shape[1]
    whole = lambda c, i: (0, 0)
    whole3 = lambda c, i: (0, 0, 0)
    grid_spec = pltpu.PrefetchScalarGridSpec(
        num_scalar_prefetch=1,
        grid=(1,),
        in_specs=[
            pl.BlockSpec((count * frames, depth), whole),
            pl.BlockSpec((HALO, strip, scans), whole3),
            pl.BlockSpec((frames, strip, scans), lambda c, i: (0, i[0], 0)),
            pl.BlockSpec((HALO, strip, scans), whole3),
            pl.BlockSpec((count, nblk, TILE, TILE), lambda c, i: (0, 0, 0, 0)),
        ],
        out_specs=[
            pl.BlockSpec((frames, strip, scans), whole3),
            pl.BlockSpec((frames, strip, scans), whole3),
        ],
        scratch_shapes=[
            pltpu.VMEM((depth, strip * scans), jnp.float32),
            pltpu.VMEM((count, rows, scans), jnp.float32),
            pltpu.VMEM((2, scans, scans), jnp.bfloat16),
            pltpu.VMEM((rows, scans), jnp.float32),
            pltpu.VMEM((rows, scans), jnp.float32),
        ],
    )
    return pl.pallas_call(
        wavelet_kernel,
        grid_spec=grid_spec,
        out_shape=[
            jax.ShapeDtypeStruct((frames, strip, scans), jnp.bfloat16),
            jax.ShapeDtypeStruct((frames, strip, scans), jnp.float32),
        ],
        compiler_params=pltpu.CompilerParams(
            dimension_semantics=("arbitrary",), vmem_limit_bytes=56 * 1024 * 1024
        ),
        interpret=interpret,
    )(first, ftab, low, slab, high, blocks)


def compute(slab, block_index, low, high, widths, interpret=False):
    frames, strip, scans = low.shape
    depth = -(-(frames + 2 * HALO) // TILE) * TILE
    scale_widths = widths.astype(jnp.float32)
    ftab = frame_tables(frames, scale_widths, depth)
    blocks = scan_blocks(scans, scale_widths)
    first = jnp.reshape(block_index, (1,)).astype(jnp.int32)
    return wavelet_core(first, ftab, low, slab, high, blocks, interpret)


def per_device(slab, widths):
    strip = slab.shape[1] // lax.axis_size("scale")
    low, high = halos(slab, strip)
    return compute(slab, lax.axis_index("scale"), low, high, widths)


def solution(mesh):
    in_specs = (P("rt", None, None), P())
    out_specs = (P("rt", "scale", None), P("rt", "scale", None))
    return jax.shard_map(
        per_device, mesh=mesh, in_specs=in_specs, out_specs=out_specs, check_vma=False
    )
```

```python
import jax
import jax.numpy as jnp
from jax import lax
from jax.experimental import pallas as pl
from jax.experimental.pallas import tpu as pltpu
from jax.sharding import PartitionSpec as P

SCAN_RATIO = 16
HALO = 24
TILE = 128


def mexican(offsets, spread):
    ratio = offsets / spread
    return (1.0 - ratio * ratio) * jnp.exp(-0.5 * ratio * ratio) / jnp.sqrt(spread)


def halos(slab, strip):
    n_scale, n_rt = lax.axis_size("scale"), lax.axis_size("rt")
    half = n_scale // 2
    s, r = lax.axis_index("scale"), lax.axis_index("rt")
    other = (s + half) % n_scale
    forward, backward = [], []
    for ss in range(n_scale):
        for rr in range(n_rt):
            flip = (ss + half) % n_scale
            if rr + 1 < n_rt:
                forward.append((ss * n_rt + rr, (ss if rr % 2 == 0 else flip) * n_rt + rr + 1))
            if rr > 0:
                backward.append((ss * n_rt + rr, (ss if rr % 2 == 1 else flip) * n_rt + rr - 1))
    frames = slab.shape[0]

    def piece(index, start):
        part = lax.dynamic_slice_in_dim(slab, index * strip, strip, axis=1)
        part = lax.slice_in_dim(part, start, start + HALO, axis=0)
        return part.astype(jnp.bfloat16)

    send_fwd = piece(jnp.where(r % 2 == 0, s, other), frames - HALO)
    send_bwd = piece(jnp.where(r % 2 == 1, s, other), 0)
    low = lax.ppermute(send_fwd, ("scale", "rt"), forward)
    high = lax.ppermute(send_bwd, ("scale", "rt"), backward)
    return low, high


def frame_tables(frames, scale_widths, depth):
    out_pos = jnp.arange(frames, dtype=jnp.float32)
    in_pos = jnp.arange(depth, dtype=jnp.float32) - HALO
    offsets = (in_pos[None, :] - out_pos[:, None])[None]
    spread = scale_widths[:, None, None]
    inside = (jnp.abs(offsets) <= HALO) & (in_pos < frames + HALO)[None, None, :]
    values = jnp.where(inside, mexican(offsets, spread), 0.0)
    return values.astype(jnp.bfloat16).reshape(-1, depth)


def scan_blocks(scans, scale_widths):
    nb = scans // TILE
    shift = jnp.arange(nb, dtype=jnp.float32) * TILE
    pos = jnp.arange(TILE, dtype=jnp.float32)
    offsets = shift[:, None, None] + (pos[:, None] - pos[None, :])[None]
    spread = SCAN_RATIO * scale_widths[:, None, None, None]
    return mexican(offsets[None], spread).astype(jnp.bfloat16)


def wavelet_kernel(strip_ref, f_ref, lo_ref, own_ref, hi_ref, b_ref, peak_ref, energy_ref,
                   p_scr, g_scr, s_scr, best_scr, total_scr):
    count, rows, scans = g_scr.shape
    frames, strip, _ = own_ref.shape
    nb = scans // TILE
    used = 2 * HALO + frames

    p_scr[used:, :] = jnp.zeros((p_scr.shape[0] - used, p_scr.shape[1]), p_scr.dtype)
    for m in range(strip):
        cols = slice(m * scans, (m + 1) * scans)
        p_scr[0:HALO, cols] = lo_ref[:, m, :]
        p_scr[HALO:HALO + frames, cols] = own_ref[:, m, :]
        p_scr[HALO + frames:used, cols] = hi_ref[:, m, :]
    fall = f_ref[...]
    for m in range(strip):
        part = p_scr[:, m * scans:(m + 1) * scans].astype(jnp.bfloat16)
        gm = jnp.dot(fall, part, preferred_element_type=jnp.float32)
        for cc in range(count):
            g_scr[cc, m * frames:(m + 1) * frames, :] = gm[cc * frames:(cc + 1) * frames, :]

    for c in range(count):
        table = s_scr.at[c % 2]
        flipped = {d: b_ref[c, d].T for d in range(1, nb)}
        for i in range(nb):
            for j in range(nb):
                block = b_ref[c, i - j] if i >= j else flipped[j - i]
                table[i * TILE:(i + 1) * TILE, j * TILE:(j + 1) * TILE] = block
        lhs = g_scr[c].astype(jnp.bfloat16)
        answer = jnp.dot(lhs, table[...], preferred_element_type=jnp.float32).astype(jnp.bfloat16)
        answer = answer.astype(jnp.float32)
        if c == 0:
            best_scr[...] = answer
            total_scr[...] = answer * answer
        else:
            best_scr[...] = jnp.maximum(best_scr[...], answer)
            total_scr[...] = total_scr[...] + answer * answer

    for m in range(strip):
        peak_ref[:, m, :] = best_scr[m * frames:(m + 1) * frames, :].astype(peak_ref.dtype)
        energy_ref[:, m, :] = total_scr[m * frames:(m + 1) * frames, :]


def wavelet_core(first, ftab, low, slab, high, blocks, interpret=False):
    count = blocks.shape[0]
    depth = ftab.shape[1]
    frames, strip, scans = low.shape
    rows = frames * strip
    nblk = blocks.shape[1]
    whole = lambda c, i: (0, 0)
    whole3 = lambda c, i: (0, 0, 0)
    grid_spec = pltpu.PrefetchScalarGridSpec(
        num_scalar_prefetch=1,
        grid=(1,),
        in_specs=[
            pl.BlockSpec((count * frames, depth), whole),
            pl.BlockSpec((HALO, strip, scans), whole3),
            pl.BlockSpec((frames, strip, scans), lambda c, i: (0, i[0], 0)),
            pl.BlockSpec((HALO, strip, scans), whole3),
            pl.BlockSpec((count, nblk, TILE, TILE), lambda c, i: (0, 0, 0, 0)),
        ],
        out_specs=[
            pl.BlockSpec((frames, strip, scans), whole3),
            pl.BlockSpec((frames, strip, scans), whole3),
        ],
        scratch_shapes=[
            pltpu.VMEM((depth, strip * scans), jnp.float32),
            pltpu.VMEM((count, rows, scans), jnp.float32),
            pltpu.VMEM((2, scans, scans), jnp.bfloat16),
            pltpu.VMEM((rows, scans), jnp.float32),
            pltpu.VMEM((rows, scans), jnp.float32),
        ],
    )
    return pl.pallas_call(
        wavelet_kernel,
        grid_spec=grid_spec,
        out_shape=[
            jax.ShapeDtypeStruct((frames, strip, scans), jnp.bfloat16),
            jax.ShapeDtypeStruct((frames, strip, scans), jnp.float32),
        ],
        compiler_params=pltpu.CompilerParams(
            dimension_semantics=("arbitrary",), vmem_limit_bytes=56 * 1024 * 1024
        ),
        interpret=interpret,
    )(first, ftab, low, slab, high, blocks)


def compute(slab, block_index, low, high, widths, interpret=False):
    frames, strip, scans = low.shape
    depth = -(-(frames + 2 * HALO) // TILE) * TILE
    scale_widths = widths.astype(jnp.float32)
    ftab = frame_tables(frames, scale_widths, depth)
    blocks = scan_blocks(scans, scale_widths)
    first = jnp.reshape(block_index, (1,)).astype(jnp.int32)
    low, high = low.astype(jnp.float32), high.astype(jnp.float32)
    return wavelet_core(first, ftab, low, slab, high, blocks, interpret)


def per_device(slab, widths):
    strip = slab.shape[1] // lax.axis_size("scale")
    low, high = halos(slab, strip)
    return compute(slab, lax.axis_index("scale"), low, high, widths)


def solution(mesh):
    in_specs = (P("rt", None, None), P())
    out_specs = (P("rt", "scale", None), P("rt", "scale", None))
    return jax.shard_map(
        per_device, mesh=mesh, in_specs=in_specs, out_specs=out_specs, check_vma=False
    )
```

```python
import jax
import jax.numpy as jnp
from jax import lax
from jax.experimental import pallas as pl
from jax.experimental.pallas import tpu as pltpu
from jax.sharding import PartitionSpec as P

SCAN_RATIO = 16
HALO = 24
TILE = 128


def mexican(offsets, spread):
    ratio = offsets / spread
    return (1.0 - ratio * ratio) * jnp.exp(-0.5 * ratio * ratio) / jnp.sqrt(spread)


def halos(slab, strip):
    n_scale, n_rt = lax.axis_size("scale"), lax.axis_size("rt")
    half = n_scale // 2
    s, r = lax.axis_index("scale"), lax.axis_index("rt")
    other = (s + half) % n_scale
    forward, backward = [], []
    for ss in range(n_scale):
        for rr in range(n_rt):
            flip = (ss + half) % n_scale
            if rr + 1 < n_rt:
                forward.append((ss * n_rt + rr, (ss if rr % 2 == 0 else flip) * n_rt + rr + 1))
            if rr > 0:
                backward.append((ss * n_rt + rr, (ss if rr % 2 == 1 else flip) * n_rt + rr - 1))
    frames = slab.shape[0]

    def piece(index, start):
        part = lax.dynamic_slice_in_dim(slab, index * strip, strip, axis=1)
        part = lax.slice_in_dim(part, start, start + HALO, axis=0)
        return part.astype(jnp.bfloat16)

    send_fwd = piece(jnp.where(r % 2 == 0, s, other), frames - HALO)
    send_bwd = piece(jnp.where(r % 2 == 1, s, other), 0)
    low = lax.ppermute(send_fwd, ("scale", "rt"), forward)
    high = lax.ppermute(send_bwd, ("scale", "rt"), backward)
    return low, high


def frame_tables(frames, scale_widths, depth):
    out_pos = jnp.arange(frames, dtype=jnp.float32)
    in_pos = jnp.arange(depth, dtype=jnp.float32) - HALO
    offsets = (in_pos[None, :] - out_pos[:, None])[None]
    spread = scale_widths[:, None, None]
    inside = (jnp.abs(offsets) <= HALO) & (in_pos < frames + HALO)[None, None, :]
    values = jnp.where(inside, mexican(offsets, spread), 0.0)
    return values.astype(jnp.bfloat16).reshape(-1, depth)


def scan_blocks(scans, scale_widths):
    nb = scans // TILE
    shift = jnp.arange(nb, dtype=jnp.float32) * TILE
    pos = jnp.arange(TILE, dtype=jnp.float32)
    offsets = shift[:, None, None] + (pos[:, None] - pos[None, :])[None]
    spread = SCAN_RATIO * scale_widths[:, None, None, None]
    return mexican(offsets[None], spread).astype(jnp.bfloat16)


def wavelet_kernel(strip_ref, f_ref, lo_ref, own_ref, hi_ref, b_ref, peak_ref, energy_ref,
                   p_scr, g_scr, s_scr, best_scr, total_scr):
    count, rows, scans = g_scr.shape
    frames, strip, _ = own_ref.shape
    nb = scans // TILE
    used = 2 * HALO + frames

    p_scr[used:, :] = jnp.zeros((p_scr.shape[0] - used, p_scr.shape[1]), p_scr.dtype)
    for m in range(strip):
        cols = slice(m * scans, (m + 1) * scans)
        p_scr[0:HALO, cols] = lo_ref[:, m, :].astype(jnp.float32)
        p_scr[HALO:HALO + frames, cols] = own_ref[:, m, :]
        p_scr[HALO + frames:used, cols] = hi_ref[:, m, :].astype(jnp.float32)
    fall = f_ref[...]
    for m in range(strip):
        part = p_scr[:, m * scans:(m + 1) * scans].astype(jnp.bfloat16)
        gm = jnp.dot(fall, part, preferred_element_type=jnp.float32)
        for cc in range(count):
            g_scr[cc, m * frames:(m + 1) * frames, :] = gm[cc * frames:(cc + 1) * frames, :]

    for c in range(count):
        table = s_scr.at[c % 2]
        flipped = {d: b_ref[c, d].T for d in range(1, nb)}
        for i in range(nb):
            for j in range(nb):
                block = b_ref[c, i - j] if i >= j else flipped[j - i]
                table[i * TILE:(i + 1) * TILE, j * TILE:(j + 1) * TILE] = block
        lhs = g_scr[c].astype(jnp.bfloat16)
        answer = jnp.dot(lhs, table[...], preferred_element_type=jnp.float32).astype(jnp.bfloat16)
        answer = answer.astype(jnp.float32)
        if c % 2 == 0 and c + 1 < count:
            held = answer
            continue
        if c % 2 == 1:
            best = jnp.maximum(held, answer)
            square = held * held + answer * answer
        else:
            best, square = answer, answer * answer
        if c < 2:
            best_scr[...] = best
            total_scr[...] = square
        else:
            best_scr[...] = jnp.maximum(best_scr[...], best)
            total_scr[...] = total_scr[...] + square

    for m in range(strip):
        peak_ref[:, m, :] = best_scr[m * frames:(m + 1) * frames, :].astype(peak_ref.dtype)
        energy_ref[:, m, :] = total_scr[m * frames:(m + 1) * frames, :]


def wavelet_core(first, ftab, low, slab, high, blocks, interpret=False):
    count = blocks.shape[0]
    depth = ftab.shape[1]
    frames, strip, scans = low.shape
    rows = frames * strip
    nblk = blocks.shape[1]
    whole = lambda c, i: (0, 0)
    whole3 = lambda c, i: (0, 0, 0)
    grid_spec = pltpu.PrefetchScalarGridSpec(
        num_scalar_prefetch=1,
        grid=(1,),
        in_specs=[
            pl.BlockSpec((count * frames, depth), whole),
            pl.BlockSpec((HALO, strip, scans), whole3),
            pl.BlockSpec((frames, strip, scans), lambda c, i: (0, i[0], 0)),
            pl.BlockSpec((HALO, strip, scans), whole3),
            pl.BlockSpec((count, nblk, TILE, TILE), lambda c, i: (0, 0, 0, 0)),
        ],
        out_specs=[
            pl.BlockSpec((frames, strip, scans), whole3),
            pl.BlockSpec((frames, strip, scans), whole3),
        ],
        scratch_shapes=[
            pltpu.VMEM((depth, strip * scans), jnp.float32),
            pltpu.VMEM((count, rows, scans), jnp.float32),
            pltpu.VMEM((2, scans, scans), jnp.bfloat16),
            pltpu.VMEM((rows, scans), jnp.float32),
            pltpu.VMEM((rows, scans), jnp.float32),
        ],
    )
    return pl.pallas_call(
        wavelet_kernel,
        grid_spec=grid_spec,
        out_shape=[
            jax.ShapeDtypeStruct((frames, strip, scans), jnp.bfloat16),
            jax.ShapeDtypeStruct((frames, strip, scans), jnp.float32),
        ],
        compiler_params=pltpu.CompilerParams(
            dimension_semantics=("arbitrary",), vmem_limit_bytes=56 * 1024 * 1024
        ),
        interpret=interpret,
    )(first, ftab, low, slab, high, blocks)


def compute(slab, block_index, low, high, widths, interpret=False):
    frames, strip, scans = low.shape
    depth = -(-(frames + 2 * HALO) // TILE) * TILE
    scale_widths = widths.astype(jnp.float32)
    ftab = frame_tables(frames, scale_widths, depth)
    blocks = scan_blocks(scans, scale_widths)
    first = jnp.reshape(block_index, (1,)).astype(jnp.int32)
    return wavelet_core(first, ftab, low, slab, high, blocks, interpret)


def per_device(slab, widths):
    strip = slab.shape[1] // lax.axis_size("scale")
    low, high = halos(slab, strip)
    return compute(slab, lax.axis_index("scale"), low, high, widths)


def solution(mesh):
    in_specs = (P("rt", None, None), P())
    out_specs = (P("rt", "scale", None), P("rt", "scale", None))
    return jax.shard_map(
        per_device, mesh=mesh, in_specs=in_specs, out_specs=out_specs, check_vma=False
    )
```

```python
import jax
import jax.numpy as jnp
from jax import lax
from jax.experimental import pallas as pl
from jax.experimental.pallas import tpu as pltpu
from jax.sharding import PartitionSpec as P

SCAN_RATIO = 16
HALO = 24
TILE = 128


def mexican(offsets, spread):
    ratio = offsets / spread
    return (1.0 - ratio * ratio) * jnp.exp(-0.5 * ratio * ratio) / jnp.sqrt(spread)


def halos(slab, strip):
    n_scale, n_rt = lax.axis_size("scale"), lax.axis_size("rt")
    half = n_scale // 2
    s, r = lax.axis_index("scale"), lax.axis_index("rt")
    other = (s + half) % n_scale
    forward, backward = [], []
    for ss in range(n_scale):
        for rr in range(n_rt):
            flip = (ss + half) % n_scale
            if rr + 1 < n_rt:
                forward.append((ss * n_rt + rr, (ss if rr % 2 == 0 else flip) * n_rt + rr + 1))
            if rr > 0:
                backward.append((ss * n_rt + rr, (ss if rr % 2 == 1 else flip) * n_rt + rr - 1))
    frames = slab.shape[0]

    def piece(index, start):
        part = lax.dynamic_slice_in_dim(slab, index * strip, strip, axis=1)
        part = lax.slice_in_dim(part, start, start + HALO, axis=0)
        return part.astype(jnp.bfloat16)

    send_fwd = piece(jnp.where(r % 2 == 0, s, other), frames - HALO)
    send_bwd = piece(jnp.where(r % 2 == 1, s, other), 0)
    low = lax.ppermute(send_fwd, ("scale", "rt"), forward)
    high = lax.ppermute(send_bwd, ("scale", "rt"), backward)
    return low, high


def frame_tables(frames, scale_widths, depth):
    out_pos = jnp.arange(frames, dtype=jnp.float32)
    in_pos = jnp.arange(depth, dtype=jnp.float32) - HALO
    offsets = (in_pos[None, :] - out_pos[:, None])[None]
    spread = scale_widths[:, None, None]
    inside = (jnp.abs(offsets) <= HALO) & (in_pos < frames + HALO)[None, None, :]
    values = jnp.where(inside, mexican(offsets, spread), 0.0)
    return values.astype(jnp.bfloat16).reshape(-1, depth)


def scan_blocks(scans, scale_widths):
    nb = scans // TILE
    shift = jnp.arange(nb, dtype=jnp.float32) * TILE
    pos = jnp.arange(TILE, dtype=jnp.float32)
    offsets = shift[:, None, None] + (pos[:, None] - pos[None, :])[None]
    spread = SCAN_RATIO * scale_widths[:, None, None, None]
    return mexican(offsets[None], spread).astype(jnp.bfloat16)


def wavelet_kernel(strip_ref, f_ref, lo_ref, own_ref, hi_ref, b_ref, peak_ref, energy_ref,
                   p_scr, g_scr, s_scr, best_scr, total_scr):
    count, rows, scans = g_scr.shape
    frames, strip, _ = own_ref.shape
    nb = scans // TILE
    used = 2 * HALO + frames

    p_scr[used:, :] = jnp.zeros((p_scr.shape[0] - used, p_scr.shape[1]), p_scr.dtype)
    for m in range(strip):
        cols = slice(m * scans, (m + 1) * scans)
        p_scr[0:HALO, cols] = lo_ref[:, m, :].astype(jnp.float32)
        p_scr[HALO:HALO + frames, cols] = own_ref[:, m, :]
        p_scr[HALO + frames:used, cols] = hi_ref[:, m, :].astype(jnp.float32)
    fall = f_ref[...]
    for m in range(strip):
        part = p_scr[:, m * scans:(m + 1) * scans].astype(jnp.bfloat16)
        gm = jnp.dot(fall, part, preferred_element_type=jnp.float32)
        for cc in range(count):
            g_scr[cc, m * frames:(m + 1) * frames, :] = gm[cc * frames:(cc + 1) * frames, :]

    for c in range(count):
        table = s_scr.at[c % 2]
        flipped = {d: b_ref[c, d].T for d in range(1, nb)}
        for i in range(nb):
            for j in range(nb):
                block = b_ref[c, i - j] if i >= j else flipped[j - i]
                table[i * TILE:(i + 1) * TILE, j * TILE:(j + 1) * TILE] = block
        lhs = g_scr[c].astype(jnp.bfloat16)
        answer = jnp.dot(lhs, table[...], preferred_element_type=jnp.float32).astype(jnp.bfloat16)
        answer = answer.astype(jnp.float32)
        if c == 0:
            best_scr[...] = answer
            total_scr[...] = answer * answer
        else:
            best_scr[...] = jnp.maximum(best_scr[...], answer)
            total_scr[...] = total_scr[...] + answer * answer

    for m in range(strip):
        peak_ref[:, m, :] = best_scr[m * frames:(m + 1) * frames, :].astype(peak_ref.dtype)
        energy_ref[:, m, :] = total_scr[m * frames:(m + 1) * frames, :]


def wavelet_core(first, ftab, low, slab, high, blocks, interpret=False):
    count = blocks.shape[0]
    depth = ftab.shape[1]
    frames, strip, scans = low.shape
    rows = frames * strip
    nblk = blocks.shape[1]
    whole = lambda c, i: (0, 0)
    whole3 = lambda c, i: (0, 0, 0)
    grid_spec = pltpu.PrefetchScalarGridSpec(
        num_scalar_prefetch=1,
        grid=(1,),
        in_specs=[
            pl.BlockSpec((count * frames, depth), whole),
            pl.BlockSpec((HALO, strip, scans), whole3),
            pl.BlockSpec((frames, strip, scans), lambda c, i: (0, i[0], 0)),
            pl.BlockSpec((HALO, strip, scans), whole3),
            pl.BlockSpec((count, nblk, TILE, TILE), lambda c, i: (0, 0, 0, 0)),
        ],
        out_specs=[
            pl.BlockSpec((frames, strip, scans), whole3),
            pl.BlockSpec((frames, strip, scans), whole3),
        ],
        scratch_shapes=[
            pltpu.VMEM((depth, strip * scans), jnp.float32),
            pltpu.VMEM((count, rows, scans), jnp.float32),
            pltpu.VMEM((2, scans, scans), jnp.bfloat16),
            pltpu.VMEM((rows, scans), jnp.float32),
            pltpu.VMEM((rows, scans), jnp.float32),
        ],
    )
    return pl.pallas_call(
        wavelet_kernel,
        grid_spec=grid_spec,
        out_shape=[
            jax.ShapeDtypeStruct((frames, strip, scans), jnp.bfloat16),
            jax.ShapeDtypeStruct((frames, strip, scans), jnp.float32),
        ],
        compiler_params=pltpu.CompilerParams(
            dimension_semantics=("arbitrary",), vmem_limit_bytes=56 * 1024 * 1024
        ),
        interpret=interpret,
    )(first, ftab, low, slab, high, blocks)


def compute(slab, block_index, low, high, widths, interpret=False):
    frames, strip, scans = low.shape
    depth = -(-(frames + 2 * HALO) // 16) * 16
    scale_widths = widths.astype(jnp.float32)
    ftab = frame_tables(frames, scale_widths, depth)
    blocks = scan_blocks(scans, scale_widths)
    first = jnp.reshape(block_index, (1,)).astype(jnp.int32)
    return wavelet_core(first, ftab, low, slab, high, blocks, interpret)


def per_device(slab, widths):
    strip = slab.shape[1] // lax.axis_size("scale")
    low, high = halos(slab, strip)
    return compute(slab, lax.axis_index("scale"), low, high, widths)


def solution(mesh):
    in_specs = (P("rt", None, None), P())
    out_specs = (P("rt", "scale", None), P("rt", "scale", None))
    return jax.shard_map(
        per_device, mesh=mesh, in_specs=in_specs, out_specs=out_specs, check_vma=False
    )
```

```python
import jax
import jax.numpy as jnp
from jax import lax
from jax.experimental import pallas as pl
from jax.experimental.pallas import tpu as pltpu
from jax.sharding import PartitionSpec as P

SCAN_RATIO = 16
HALO = 24
TILE = 128


def mexican(offsets, spread):
    ratio = offsets / spread
    return (1.0 - ratio * ratio) * jnp.exp(-0.5 * ratio * ratio) / jnp.sqrt(spread)


def halos(slab, strip):
    n_scale, n_rt = lax.axis_size("scale"), lax.axis_size("rt")
    half = n_scale // 2
    s, r = lax.axis_index("scale"), lax.axis_index("rt")
    other = (s + half) % n_scale
    forward, backward = [], []
    for ss in range(n_scale):
        for rr in range(n_rt):
            flip = (ss + half) % n_scale
            if rr + 1 < n_rt:
                forward.append((ss * n_rt + rr, (ss if rr % 2 == 0 else flip) * n_rt + rr + 1))
            if rr > 0:
                backward.append((ss * n_rt + rr, (ss if rr % 2 == 1 else flip) * n_rt + rr - 1))
    frames = slab.shape[0]

    def piece(index, start):
        part = lax.dynamic_slice_in_dim(slab, index * strip, strip, axis=1)
        part = lax.slice_in_dim(part, start, start + HALO, axis=0)
        return part.astype(jnp.bfloat16)

    send_fwd = piece(jnp.where(r % 2 == 0, s, other), frames - HALO)
    send_bwd = piece(jnp.where(r % 2 == 1, s, other), 0)
    low = lax.ppermute(send_fwd, ("scale", "rt"), forward)
    high = lax.ppermute(send_bwd, ("scale", "rt"), backward)
    return low, high


def frame_tables(frames, scale_widths, depth):
    out_pos = jnp.arange(frames, dtype=jnp.float32)
    in_pos = jnp.arange(depth, dtype=jnp.float32) - HALO
    offsets = (in_pos[None, :] - out_pos[:, None])[None]
    spread = scale_widths[:, None, None]
    inside = (jnp.abs(offsets) <= HALO) & (in_pos < frames + HALO)[None, None, :]
    values = jnp.where(inside, mexican(offsets, spread), 0.0)
    return values.astype(jnp.bfloat16).reshape(-1, depth)


def scan_blocks(scans, scale_widths):
    nb = scans // TILE
    shift = jnp.arange(nb, dtype=jnp.float32) * TILE
    pos = jnp.arange(TILE, dtype=jnp.float32)
    offsets = shift[:, None, None] + (pos[:, None] - pos[None, :])[None]
    spread = SCAN_RATIO * scale_widths[:, None, None, None]
    return mexican(offsets[None], spread).astype(jnp.bfloat16)


def wavelet_kernel(strip_ref, f_ref, lo_ref, own_ref, hi_ref, b_ref, peak_ref, energy_ref,
                   p_scr, g_scr, s_scr, best_scr, total_scr):
    count, rows, scans = g_scr.shape
    frames, strip, _ = own_ref.shape
    nb = scans // TILE
    used = 2 * HALO + frames

    p_scr[used:, :] = jnp.zeros((p_scr.shape[0] - used, p_scr.shape[1]), p_scr.dtype)
    for m in range(strip):
        cols = slice(m * scans, (m + 1) * scans)
        p_scr[0:HALO, cols] = lo_ref[:, m, :].astype(jnp.float32)
        p_scr[HALO:HALO + frames, cols] = own_ref[:, m, :]
        p_scr[HALO + frames:used, cols] = hi_ref[:, m, :].astype(jnp.float32)
    g_all = jnp.dot(f_ref[...], p_scr[...].astype(jnp.bfloat16), preferred_element_type=jnp.float32)
    for m in range(strip):
        for cc in range(count):
            g_scr[cc, m * frames:(m + 1) * frames, :] = g_all[cc * frames:(cc + 1) * frames, m * scans:(m + 1) * scans]

    for c in range(count):
        table = s_scr.at[c % 2]
        flipped = {d: b_ref[c, d].T for d in range(1, nb)}
        for i in range(nb):
            for j in range(nb):
                block = b_ref[c, i - j] if i >= j else flipped[j - i]
                table[i * TILE:(i + 1) * TILE, j * TILE:(j + 1) * TILE] = block
        lhs = g_scr[c].astype(jnp.bfloat16)
        answer = jnp.dot(lhs, table[...], preferred_element_type=jnp.float32).astype(jnp.bfloat16)
        answer = answer.astype(jnp.float32)
        if c == 0:
            best_scr[...] = answer
            total_scr[...] = answer * answer
        else:
            best_scr[...] = jnp.maximum(best_scr[...], answer)
            total_scr[...] = total_scr[...] + answer * answer

    for m in range(strip):
        peak_ref[:, m, :] = best_scr[m * frames:(m + 1) * frames, :].astype(peak_ref.dtype)
        energy_ref[:, m, :] = total_scr[m * frames:(m + 1) * frames, :]


def wavelet_core(first, ftab, low, slab, high, blocks, interpret=False):
    count = blocks.shape[0]
    depth = ftab.shape[1]
    frames, strip, scans = low.shape
    rows = frames * strip
    nblk = blocks.shape[1]
    whole = lambda c, i: (0, 0)
    whole3 = lambda c, i: (0, 0, 0)
    grid_spec = pltpu.PrefetchScalarGridSpec(
        num_scalar_prefetch=1,
        grid=(1,),
        in_specs=[
            pl.BlockSpec((count * frames, depth), whole),
            pl.BlockSpec((HALO, strip, scans), whole3),
            pl.BlockSpec((frames, strip, scans), lambda c, i: (0, i[0], 0)),
            pl.BlockSpec((HALO, strip, scans), whole3),
            pl.BlockSpec((count, nblk, TILE, TILE), lambda c, i: (0, 0, 0, 0)),
        ],
        out_specs=[
            pl.BlockSpec((frames, strip, scans), whole3),
            pl.BlockSpec((frames, strip, scans), whole3),
        ],
        scratch_shapes=[
            pltpu.VMEM((depth, strip * scans), jnp.float32),
            pltpu.VMEM((count, rows, scans), jnp.float32),
            pltpu.VMEM((2, scans, scans), jnp.bfloat16),
            pltpu.VMEM((rows, scans), jnp.float32),
            pltpu.VMEM((rows, scans), jnp.float32),
        ],
    )
    return pl.pallas_call(
        wavelet_kernel,
        grid_spec=grid_spec,
        out_shape=[
            jax.ShapeDtypeStruct((frames, strip, scans), jnp.bfloat16),
            jax.ShapeDtypeStruct((frames, strip, scans), jnp.float32),
        ],
        compiler_params=pltpu.CompilerParams(
            dimension_semantics=("arbitrary",), vmem_limit_bytes=56 * 1024 * 1024
        ),
        interpret=interpret,
    )(first, ftab, low, slab, high, blocks)


def compute(slab, block_index, low, high, widths, interpret=False):
    frames, strip, scans = low.shape
    depth = -(-(frames + 2 * HALO) // 16) * 16
    scale_widths = widths.astype(jnp.float32)
    ftab = frame_tables(frames, scale_widths, depth)
    blocks = scan_blocks(scans, scale_widths)
    first = jnp.reshape(block_index, (1,)).astype(jnp.int32)
    return wavelet_core(first, ftab, low, slab, high, blocks, interpret)


def per_device(slab, widths):
    strip = slab.shape[1] // lax.axis_size("scale")
    low, high = halos(slab, strip)
    return compute(slab, lax.axis_index("scale"), low, high, widths)


def solution(mesh):
    in_specs = (P("rt", None, None), P())
    out_specs = (P("rt", "scale", None), P("rt", "scale", None))
    return jax.shard_map(
        per_device, mesh=mesh, in_specs=in_specs, out_specs=out_specs, check_vma=False
    )
```

```python
import jax
import jax.numpy as jnp
from jax import lax
from jax.experimental import pallas as pl
from jax.experimental.pallas import tpu as pltpu
from jax.sharding import PartitionSpec as P

SCAN_RATIO = 16
HALO = 24
TILE = 128


def mexican(offsets, spread):
    ratio = offsets / spread
    return (1.0 - ratio * ratio) * jnp.exp(-0.5 * ratio * ratio) / jnp.sqrt(spread)


def halos(slab, strip):
    n_scale, n_rt = lax.axis_size("scale"), lax.axis_size("rt")
    half = n_scale // 2
    s, r = lax.axis_index("scale"), lax.axis_index("rt")
    other = (s + half) % n_scale
    forward, backward = [], []
    for ss in range(n_scale):
        for rr in range(n_rt):
            flip = (ss + half) % n_scale
            if rr + 1 < n_rt:
                forward.append((ss * n_rt + rr, (ss if rr % 2 == 0 else flip) * n_rt + rr + 1))
            if rr > 0:
                backward.append((ss * n_rt + rr, (ss if rr % 2 == 1 else flip) * n_rt + rr - 1))
    frames = slab.shape[0]

    def piece(index, start):
        part = lax.dynamic_slice_in_dim(slab, index * strip, strip, axis=1)
        part = lax.slice_in_dim(part, start, start + HALO, axis=0)
        return part.astype(jnp.bfloat16)

    send_fwd = piece(jnp.where(r % 2 == 0, s, other), frames - HALO)
    send_bwd = piece(jnp.where(r % 2 == 1, s, other), 0)
    low = lax.ppermute(send_fwd, ("scale", "rt"), forward)
    high = lax.ppermute(send_bwd, ("scale", "rt"), backward)
    return low, high


def frame_tables(frames, scale_widths, depth):
    out_pos = jnp.arange(frames, dtype=jnp.float32)
    in_pos = jnp.arange(depth, dtype=jnp.float32) - HALO
    offsets = (in_pos[None, :] - out_pos[:, None])[None]
    spread = scale_widths[:, None, None]
    inside = (jnp.abs(offsets) <= HALO) & (in_pos < frames + HALO)[None, None, :]
    values = jnp.where(inside, mexican(offsets, spread), 0.0)
    return values.astype(jnp.bfloat16).reshape(-1, depth)


def scan_blocks(scans, scale_widths):
    nb = scans // TILE
    shift = jnp.arange(nb, dtype=jnp.float32) * TILE
    pos = jnp.arange(TILE, dtype=jnp.float32)
    offsets = shift[:, None, None] + (pos[:, None] - pos[None, :])[None]
    spread = SCAN_RATIO * scale_widths[:, None, None, None]
    return mexican(offsets[None], spread).astype(jnp.bfloat16)


def wavelet_kernel(strip_ref, f_ref, lo_ref, own_ref, hi_ref, b_hbm, peak_ref, energy_ref,
                   b_ref, sem, p_scr, g_scr, s_scr, best_scr, total_scr):
    count, rows, scans = g_scr.shape
    frames, strip, _ = own_ref.shape
    nb = scans // TILE
    used = 2 * HALO + frames
    tables = pltpu.make_async_copy(b_hbm, b_ref, sem.at[0])
    tables.start()

    p_scr[used:, :] = jnp.zeros((p_scr.shape[0] - used, p_scr.shape[1]), p_scr.dtype)
    for m in range(strip):
        cols = slice(m * scans, (m + 1) * scans)
        p_scr[0:HALO, cols] = lo_ref[:, m, :].astype(jnp.float32)
        p_scr[HALO:HALO + frames, cols] = own_ref[:, m, :]
        p_scr[HALO + frames:used, cols] = hi_ref[:, m, :].astype(jnp.float32)
    fall = f_ref[...]
    for m in range(strip):
        part = p_scr[:, m * scans:(m + 1) * scans].astype(jnp.bfloat16)
        gm = jnp.dot(fall, part, preferred_element_type=jnp.float32)
        for cc in range(count):
            g_scr[cc, m * frames:(m + 1) * frames, :] = gm[cc * frames:(cc + 1) * frames, :]

    tables.wait()
    for c in range(count):
        table = s_scr.at[c % 2]
        flipped = {d: b_ref[c, d].T for d in range(1, nb)}
        for i in range(nb):
            for j in range(nb):
                block = b_ref[c, i - j] if i >= j else flipped[j - i]
                table[i * TILE:(i + 1) * TILE, j * TILE:(j + 1) * TILE] = block
        lhs = g_scr[c].astype(jnp.bfloat16)
        answer = jnp.dot(lhs, table[...], preferred_element_type=jnp.float32).astype(jnp.bfloat16)
        answer = answer.astype(jnp.float32)
        if c == 0:
            best_scr[...] = answer
            total_scr[...] = answer * answer
        else:
            best_scr[...] = jnp.maximum(best_scr[...], answer)
            total_scr[...] = total_scr[...] + answer * answer

    for m in range(strip):
        peak_ref[:, m, :] = best_scr[m * frames:(m + 1) * frames, :].astype(peak_ref.dtype)
        energy_ref[:, m, :] = total_scr[m * frames:(m + 1) * frames, :]


def wavelet_core(first, ftab, low, slab, high, blocks, interpret=False):
    count = blocks.shape[0]
    depth = ftab.shape[1]
    frames, strip, scans = low.shape
    rows = frames * strip
    nblk = blocks.shape[1]
    whole = lambda c, i: (0, 0)
    whole3 = lambda c, i: (0, 0, 0)
    grid_spec = pltpu.PrefetchScalarGridSpec(
        num_scalar_prefetch=1,
        grid=(1,),
        in_specs=[
            pl.BlockSpec((count * frames, depth), whole),
            pl.BlockSpec((HALO, strip, scans), whole3),
            pl.BlockSpec((frames, strip, scans), lambda c, i: (0, i[0], 0)),
            pl.BlockSpec((HALO, strip, scans), whole3),
            pl.BlockSpec(memory_space=pl.ANY),
        ],
        out_specs=[
            pl.BlockSpec((frames, strip, scans), whole3),
            pl.BlockSpec((frames, strip, scans), whole3),
        ],
        scratch_shapes=[
            pltpu.VMEM(blocks.shape, blocks.dtype),
            pltpu.SemaphoreType.DMA((1,)),
            pltpu.VMEM((depth, strip * scans), jnp.float32),
            pltpu.VMEM((count, rows, scans), jnp.float32),
            pltpu.VMEM((2, scans, scans), jnp.bfloat16),
            pltpu.VMEM((rows, scans), jnp.float32),
            pltpu.VMEM((rows, scans), jnp.float32),
        ],
    )
    return pl.pallas_call(
        wavelet_kernel,
        grid_spec=grid_spec,
        out_shape=[
            jax.ShapeDtypeStruct((frames, strip, scans), jnp.bfloat16),
            jax.ShapeDtypeStruct((frames, strip, scans), jnp.float32),
        ],
        compiler_params=pltpu.CompilerParams(
            dimension_semantics=("arbitrary",), vmem_limit_bytes=56 * 1024 * 1024
        ),
        interpret=interpret,
    )(first, ftab, low, slab, high, blocks)


def compute(slab, block_index, low, high, widths, interpret=False):
    frames, strip, scans = low.shape
    depth = -(-(frames + 2 * HALO) // TILE) * TILE
    scale_widths = widths.astype(jnp.float32)
    ftab = frame_tables(frames, scale_widths, depth)
    blocks = scan_blocks(scans, scale_widths)
    first = jnp.reshape(block_index, (1,)).astype(jnp.int32)
    return wavelet_core(first, ftab, low, slab, high, blocks, interpret)


def per_device(slab, widths):
    strip = slab.shape[1] // lax.axis_size("scale")
    low, high = halos(slab, strip)
    return compute(slab, lax.axis_index("scale"), low, high, widths)


def solution(mesh):
    in_specs = (P("rt", None, None), P())
    out_specs = (P("rt", "scale", None), P("rt", "scale", None))
    return jax.shard_map(
        per_device, mesh=mesh, in_specs=in_specs, out_specs=out_specs, check_vma=False
    )
```
